32 devices in a mesh: clique: 8 (over z, core), shard: 4 (over y, x).
Axes of the slice: x: 2, y: 2, z: 4, core: 2. Of those that a mesh axis runs over, the one named last changes fastest.
Arguments:
- tables: float32 [3, 8, 4096, 128], P(None, 'clique', 'shard'), may hold values from 0.1 to 10
- up_map: int32 [2, 8, 4096], P(None, 'clique', 'shard'), may hold values from 0 to 4095, as said below
- down_map: int32 [2, 8, 4096], P(None, 'clique', 'shard'), may hold values from 0 to 4095, as said below
- parents: int32 [2, 8], replicated, may hold values from 0 to 7
Outputs:
- calibrated: float32 [3, 8, 4096, 128], P(None, 'clique', 'shard')
The draws below stay inside these ranges and needn't reach their ends.
Inputs may be any that keep to these rules, and one draw needn't show every extreme that they name: For every edge and clique, of the 1024 blocks of one device exactly 256 name blocks in each range [k * 1024, (k + 1) * 1024). Every list of up_map and down_map names the same set of separator blocks; a named separator block is named by the same number of blocks of a clique in every list, a multiple of 1. For every edge and clique, of the 1024 blocks of one device exactly 256 name blocks in each range [k * 1024, (k + 1) * 1024). Every list of up_map and down_map names the same set of separator blocks; a named separator block is named by the same number of blocks of a clique in every list, a multiple of 1.
All inputs are finite; a program needn't handle non-finite values.
Results may differ from the reference program's by a relative error of at most 0.0003.
Values sent between devices are 32-bit elements; how exact they have to be, the bound alone decides.
No kernel may reach another device: no remote copies, remote signals or barrier semaphores. Data moves between devices by JAX's collectives and lax.ppermute only.
A program may use at most 64 MiB of HBM per device.

```python
import math
import jax
import jax.numpy as jnp
import numpy as np
from jax import lax

SEPB = 4096
LANES = 128
BLK_DEV = 1024
LEVELS = 3
EDGES = 2
CLIQUES = 8
BLOCKS = 4096


def separator_lists(key, common_key):
    shards = BLOCKS // BLK_DEV
    per_peer = BLK_DEV // shards
    per_owner = SEPB // shards
    grouping = jax.random.randint(common_key, (shards, per_owner), 0, per_owner, dtype=jnp.int32)

    def one_clique(clique_key):
        first, second = jax.random.split(clique_key)
        owner_keys = jax.random.split(first, shards)
        slots = jax.vmap(lambda subkey: jax.random.permutation(subkey, BLK_DEV))(owner_keys) % per_owner
        slots = jnp.take_along_axis(grouping, slots.astype(jnp.int32), axis=1)
        named = slots + (jnp.arange(shards, dtype=jnp.int32) * per_owner)[:, None]
        named = named.reshape(shards, shards, per_peer).transpose(1, 0, 2).reshape(shards, BLK_DEV)
        order_keys = jax.random.split(second, shards)
        orders = jax.vmap(lambda subkey: jax.random.permutation(subkey, BLK_DEV))(order_keys)
        named = jnp.take_along_axis(named, orders, axis=1)
        return named.reshape(BLOCKS)
    keys = jax.random.split(key, EDGES * CLIQUES)
    return jax.vmap(one_clique)(keys).reshape(EDGES, CLIQUES, BLOCKS).astype(jnp.int32)


def draw_up_map(key, part):
    return separator_lists(jax.random.fold_in(key, 11), jax.random.fold_in(key, 37))


def draw_down_map(key, part):
    return separator_lists(jax.random.fold_in(key, 23), jax.random.fold_in(key, 37))


def place_ends(array, stream_key, least, high):
    extent = array.shape
    place = [jax.random.randint(jax.random.fold_in(stream_key, axis), (), 0, extent[axis]) for axis in range(len(extent))]
    array = array.at[tuple(place)].set(least)
    longest = extent.index(max(extent))
    place[longest] = (place[longest] + 1) % extent[longest]
    return array.at[tuple(place)].set(high)


def steps_of(key, dims, cuts, smallest, high):
    def one(dim, blocks):
        heights = jax.random.uniform(jax.random.fold_in(jax.random.fold_in(key, 6), dim), (blocks,), jnp.float32, smallest / len(cuts), high / len(cuts))
        return jnp.repeat(jnp.exp(heights), dims[dim] // blocks).reshape((-1,) + (1,) * (len(dims) - dim - 1))

    gain = one(*cuts[0])
    for cut in cuts[1:]:
        gain = gain * one(*cut)
    return gain


def rank_table(number_of, skew):
    portions = [(1 << 20) // math.isqrt(standing ** skew) + 1 for standing in range(1, number_of + 1)]
    width = 1 + sum(portions) // (1 << 30)
    return np.cumsum(np.array([max(1, weight // width) for weight in portions]))


def skewed_ids(key, shape, amount, slope):
    grid = rank_table(amount, slope)
    lot = jax.random.randint(jax.random.fold_in(key, 1), shape, 0, int(grid[amount - 1]))
    grade = jnp.searchsorted(jnp.asarray(grid, jnp.int32), lot, side="right")
    return jax.random.permutation(jax.random.fold_in(key, 2), amount)[grade].astype(jnp.int32)


def setup_inputs(seed: int = 0) -> dict:
    key_list = jax.random.split(jax.random.key(seed), 5)
    return {
        "tables": jnp.clip(jnp.exp(math.log(10.0) - 4.6051702 * jax.random.uniform(key_list[0], (LEVELS, CLIQUES, BLOCKS, LANES), jnp.float32) ** steps_of(key_list[0], (LEVELS, CLIQUES, BLOCKS, LANES), ((1, 8), (2, 4)), -0.2, 0.2)), 0.1, 10.0),
        "up_map": draw_up_map(jax.random.fold_in(key_list[4], 71), 0),
        "down_map": draw_down_map(jax.random.fold_in(key_list[4], 71), 0),
        "parents": place_ends(skewed_ids(key_list[3], (EDGES, CLIQUES), CLIQUES, 2), jax.random.fold_in(key_list[3], 3), 0, CLIQUES - 1).astype(jnp.int32),
    }


def scaled_message(potential, index_list):
    message = jax.ops.segment_sum(potential, index_list, num_segments=SEPB)
    factor = (SEPB * LANES) / jnp.sum(message)
    return message * factor


def pick_rows(source_rows, index_list):
    return source_rows[index_list]


def reference(tables, up_map, down_map, parents):
    current = [tables[0], tables[1], tables[2]]
    previous = [tables[0], tables[0]]
    clique_ids = jnp.arange(CLIQUES, dtype=jnp.int32)
    for edge in (1, 0):
        selector = (parents[edge][:, None] == clique_ids[None, :]).astype(jnp.float32)
        scaled = jax.vmap(scaled_message)(current[edge + 1], up_map[edge])
        previous[edge] = scaled
        summed = jnp.einsum("cp,csl->psl", selector, jnp.log(scaled), precision=lax.Precision.HIGHEST)
        incoming = jnp.exp(summed)
        current[edge] = current[edge] * jax.vmap(pick_rows)(incoming, down_map[edge])
    for edge in (0, 1):
        fresh = jax.vmap(scaled_message)(current[edge], down_map[edge])
        update = fresh[parents[edge]] / previous[edge]
        current[edge + 1] = current[edge + 1] * jax.vmap(pick_rows)(update, up_map[edge])
    return jnp.stack(current)
```

```python
import jax
import jax.numpy as jnp
from jax import lax
from jax.sharding import PartitionSpec as P

SEPB = 4096
PAD = 8


def split_dot(one_hot, x):
    lanes = x.shape[-1]
    hi = lax.reduce_precision(x, exponent_bits=8, mantissa_bits=7)
    rest = x - hi
    mid = lax.reduce_precision(rest, exponent_bits=8, mantissa_bits=7)
    lo = rest - mid
    parts = jnp.concatenate([hi, mid, lo], axis=1).astype(jnp.bfloat16)
    y = jnp.dot(
        one_hot,
        parts,
        preferred_element_type=jnp.float32,
    )
    return (y[:, :lanes] + y[:, lanes : 2 * lanes]) + y[:, 2 * lanes :]


def gather_rows(x, index):
    one_hot = (index[:, None] == jnp.arange(x.shape[0], dtype=jnp.int32)[None, :]).astype(
        jnp.bfloat16
    )
    return split_dot(one_hot, x)


def segment_rows(x, segment, count):
    one_hot = (jnp.arange(count, dtype=jnp.int32)[:, None] == segment[None, :]).astype(
        jnp.bfloat16
    )
    return split_dot(one_hot, x)


def shards(tables, up_map, down_map, parents):
    shard_count = lax.axis_size("shard")
    clique_count = lax.axis_size("clique")
    block_count = tables.shape[2]
    lane_count = tables.shape[3]
    per_owner = SEPB // shard_count
    per_peer = block_count // shard_count
    sep_states = float(SEPB * lane_count)

    lists = jnp.stack([up_map[1, 0], up_map[0, 0], down_map[0, 0], down_map[1, 0]])
    owner = lists // per_owner
    slot = lists % per_owner
    order = jnp.argsort(owner, axis=1, stable=True)
    sent_slots = jnp.take_along_axis(slot, order, axis=1).reshape(4, shard_count, per_peer)
    arrived = lax.all_to_all(sent_slots, "shard", 1, 1, tiled=True).reshape(4, block_count)
    is_owner = owner[:, :, None] == jnp.arange(shard_count, dtype=jnp.int32)[None, None, :]
    rank = jnp.sum(jnp.where(is_owner, jnp.cumsum(is_owner.astype(jnp.int32), axis=1), 0), axis=2)
    position = owner * per_peer + rank - 1

    def send(sorted_rows, which):
        partial_sum = jnp.sum(sorted_rows)
        payload = jnp.concatenate(
            [
                sorted_rows.reshape(shard_count, per_peer, lane_count),
                jnp.broadcast_to(partial_sum, (shard_count, PAD, lane_count)),
            ],
            axis=1,
        )
        arrived_rows = lax.all_to_all(payload, "shard", 0, 0, tiled=True)
        total = jnp.sum(arrived_rows[:, per_peer, 0])
        rows = arrived_rows[:, :per_peer].reshape(block_count, lane_count)
        message = segment_rows(rows, arrived[which], per_owner)
        return message * (sep_states / total)

    def fetch(owned_rows, which):
        owned_rows = jnp.where(jnp.isfinite(owned_rows), owned_rows, 0.0)
        picked = gather_rows(owned_rows, arrived[which])
        back = lax.all_to_all(
            picked.reshape(shard_count, per_peer, lane_count), "shard", 0, 0, tiled=True
        )
        return back.reshape(block_count, lane_count)

    def route(owned_rows, mixing):
        pieces = owned_rows.reshape(clique_count, per_owner // clique_count, lane_count)
        combined = jnp.einsum(
            "oi,ixl->oxl",
            mixing,
            lax.all_to_all(pieces, "clique", split_axis=0, concat_axis=0, tiled=True),
            precision=lax.Precision.HIGHEST,
        )
        moved = lax.all_to_all(combined, "clique", split_axis=0, concat_axis=0, tiled=True)
        return moved.reshape(per_owner, lane_count)

    clique_ids = jnp.arange(clique_count, dtype=jnp.int32)
    sel = [
        (parents[edge][:, None] == clique_ids[None, :]).astype(jnp.float32) for edge in (0, 1)
    ]
    t0, t1, t2 = tables[0, 0], tables[1, 0], tables[2, 0]

    t2_up1 = gather_rows(t2, order[0])
    scaled1 = send(t2_up1, 0)
    incoming1 = jnp.exp(route(jnp.log(scaled1), sel[1].T))
    t1_down1 = gather_rows(t1, order[3]) * fetch(incoming1, 3)
    t1_up0 = gather_rows(t1_down1, jnp.take(position[3], order[1]))
    scaled0 = send(t1_up0, 1)
    incoming0 = jnp.exp(route(jnp.log(scaled0), sel[0].T))
    t0_down0 = gather_rows(t0, order[2]) * fetch(incoming0, 2)
    out0 = gather_rows(t0_down0, position[2])
    fresh0 = send(t0_down0, 2)
    update0 = route(fresh0, sel[0]) / scaled0
    t1_up0 = t1_up0 * fetch(update0, 1)
    out1 = gather_rows(t1_up0, position[1])
    t1_down1 = gather_rows(t1_up0, jnp.take(position[1], order[3]))
    fresh1 = send(t1_down1, 3)
    update1 = route(fresh1, sel[1]) / scaled1
    t2_up1 = t2_up1 * fetch(update1, 0)
    out2 = gather_rows(t2_up1, position[0])
    return jnp.stack([out0, out1, out2])[:, None]


def solution(mesh):
    return jax.shard_map(
        shards,
        mesh=mesh,
        in_specs=(
            P(None, "clique", "shard", None),
            P(None, "clique", "shard"),
            P(None, "clique", "shard"),
            P(),
        ),
        out_specs=P(None, "clique", "shard", None),
        check_vma=False,
    )
```

```python
import jax
import jax.numpy as jnp
from jax import lax
from jax.sharding import PartitionSpec as P

SEPB = 4096
PAD = 8


def split_dot(one_hot, x):
    lanes = x.shape[-1]
    hi = lax.reduce_precision(x, exponent_bits=8, mantissa_bits=7)
    rest = x - hi
    mid = lax.reduce_precision(rest, exponent_bits=8, mantissa_bits=7)
    lo = rest - mid
    parts = jnp.concatenate([hi, mid, lo], axis=1).astype(jnp.bfloat16)
    y = jnp.dot(
        one_hot,
        parts,
        preferred_element_type=jnp.float32,
    )
    return (y[:, :lanes] + y[:, lanes : 2 * lanes]) + y[:, 2 * lanes :]


def gather_rows(x, index):
    one_hot = (index[:, None] == jnp.arange(x.shape[0], dtype=jnp.int32)[None, :]).astype(
        jnp.bfloat16
    )
    return split_dot(one_hot, x)


def segment_rows(x, segment, count):
    one_hot = (jnp.arange(count, dtype=jnp.int32)[:, None] == segment[None, :]).astype(
        jnp.bfloat16
    )
    return split_dot(one_hot, x)


def shards(tables, up_map, down_map, parents):
    shard_count = lax.axis_size("shard")
    clique_count = lax.axis_size("clique")
    block_count = tables.shape[2]
    lane_count = tables.shape[3]
    per_owner = SEPB // shard_count
    per_peer = block_count // shard_count
    sep_states = float(SEPB * lane_count)

    lists = jnp.stack([up_map[1, 0], up_map[0, 0], down_map[0, 0], down_map[1, 0]])
    owner = lists // per_owner
    slot = lists % per_owner
    blocks = jnp.broadcast_to(jnp.arange(block_count, dtype=jnp.int32), lists.shape)
    _, sent_slots, order = lax.sort((owner, slot, blocks), dimension=1, num_keys=1, is_stable=True)
    arrived = lax.all_to_all(
        sent_slots.reshape(4, shard_count, per_peer), "shard", 1, 1, tiled=True
    ).reshape(4, block_count)
    position = lax.sort((order, blocks), dimension=1, num_keys=1)[1]
    moves = lax.sort(
        (jnp.stack([position[1], position[3]]), jnp.stack([position[3], position[1]])),
        dimension=1,
        num_keys=1,
    )[1]

    def send(sorted_rows, which):
        partial_sum = jnp.sum(sorted_rows)
        payload = jnp.concatenate(
            [
                sorted_rows.reshape(shard_count, per_peer, lane_count),
                jnp.broadcast_to(partial_sum, (shard_count, PAD, lane_count)),
            ],
            axis=1,
        )
        arrived_rows = lax.all_to_all(payload, "shard", 0, 0, tiled=True)
        total = jnp.sum(arrived_rows[:, per_peer, 0])
        rows = arrived_rows[:, :per_peer].reshape(block_count, lane_count)
        message = segment_rows(rows, arrived[which], per_owner)
        return message * (sep_states / total)

    def fetch(owned_rows, which):
        owned_rows = jnp.where(jnp.isfinite(owned_rows), owned_rows, 0.0)
        picked = gather_rows(owned_rows, arrived[which])
        back = lax.all_to_all(
            picked.reshape(shard_count, per_peer, lane_count), "shard", 0, 0, tiled=True
        )
        return back.reshape(block_count, lane_count)

    def route(owned_rows, mixing):
        pieces = owned_rows.reshape(clique_count, per_owner // clique_count, lane_count)
        combined = jnp.einsum(
            "oi,ixl->oxl",
            mixing,
            lax.all_to_all(pieces, "clique", split_axis=0, concat_axis=0, tiled=True),
            precision=lax.Precision.HIGHEST,
        )
        moved = lax.all_to_all(combined, "clique", split_axis=0, concat_axis=0, tiled=True)
        return moved.reshape(per_owner, lane_count)

    clique_ids = jnp.arange(clique_count, dtype=jnp.int32)
    sel = [
        (parents[edge][:, None] == clique_ids[None, :]).astype(jnp.float32) for edge in (0, 1)
    ]
    t0, t1, t2 = tables[0, 0], tables[1, 0], tables[2, 0]

    t2_up1 = gather_rows(t2, order[0])
    scaled1 = send(t2_up1, 0)
    incoming1 = jnp.exp(route(jnp.log(scaled1), sel[1].T))
    t1_down1 = gather_rows(t1, order[3]) * fetch(incoming1, 3)
    t1_up0 = gather_rows(t1_down1, moves[0])
    scaled0 = send(t1_up0, 1)
    incoming0 = jnp.exp(route(jnp.log(scaled0), sel[0].T))
    t0_down0 = gather_rows(t0, order[2]) * fetch(incoming0, 2)
    out0 = gather_rows(t0_down0, position[2])
    fresh0 = send(t0_down0, 2)
    update0 = route(fresh0, sel[0]) / scaled0
    t1_up0 = t1_up0 * fetch(update0, 1)
    out1 = gather_rows(t1_up0, position[1])
    t1_down1 = gather_rows(t1_up0, moves[1])
    fresh1 = send(t1_down1, 3)
    update1 = route(fresh1, sel[1]) / scaled1
    t2_up1 = t2_up1 * fetch(update1, 0)
    out2 = gather_rows(t2_up1, position[0])
    return jnp.stack([out0, out1, out2])[:, None]


def solution(mesh):
    return jax.shard_map(
        shards,
        mesh=mesh,
        in_specs=(
            P(None, "clique", "shard", None),
            P(None, "clique", "shard"),
            P(None, "clique", "shard"),
            P(),
        ),
        out_specs=P(None, "clique", "shard", None),
        check_vma=False,
    )
```

```python
import jax
import jax.numpy as jnp
from jax import lax
from jax.sharding import PartitionSpec as P

SEPB = 4096
PAD = 8


def split_dot(one_hot, x):
    lanes = x.shape[-1]
    hi = lax.reduce_precision(x, exponent_bits=8, mantissa_bits=7)
    rest = x - hi
    mid = lax.reduce_precision(rest, exponent_bits=8, mantissa_bits=7)
    lo = rest - mid
    parts = jnp.concatenate([hi, mid, lo], axis=1).astype(jnp.bfloat16)
    y = jnp.dot(
        one_hot,
        parts,
        preferred_element_type=jnp.float32,
    )
    return (y[:, :lanes] + y[:, lanes : 2 * lanes]) + y[:, 2 * lanes :]


def gather_rows(x, index):
    one_hot = (index[:, None] == jnp.arange(x.shape[0], dtype=jnp.int32)[None, :]).astype(
        jnp.bfloat16
    )
    return split_dot(one_hot, x)


def segment_rows(x, segment, count):
    one_hot = (jnp.arange(count, dtype=jnp.int32)[:, None] == segment[None, :]).astype(
        jnp.bfloat16
    )
    return split_dot(one_hot, x)


def shards(tables, up_map, down_map, parents):
    shard_count = lax.axis_size("shard")
    clique_count = lax.axis_size("clique")
    block_count = tables.shape[2]
    lane_count = tables.shape[3]
    per_owner = SEPB // shard_count
    per_peer = block_count // shard_count
    sep_states = float(SEPB * lane_count)

    lists = jnp.stack([up_map[1, 0], up_map[0, 0], down_map[0, 0], down_map[1, 0]])
    owner = lists // per_owner
    slot = lists % per_owner
    blocks = jnp.broadcast_to(jnp.arange(block_count, dtype=jnp.int32), lists.shape)
    _, sent_slots, order = lax.sort((owner, slot, blocks), dimension=1, num_keys=1, is_stable=True)
    arrived = lax.all_to_all(
        sent_slots.reshape(4, shard_count, per_peer), "shard", 1, 1, tiled=True
    ).reshape(4, block_count)
    position = lax.sort((order, blocks), dimension=1, num_keys=1)[1]
    moves = lax.sort(
        (jnp.stack([position[1], position[3]]), jnp.stack([position[3], position[1]])),
        dimension=1,
        num_keys=1,
    )[1]

    def send(sorted_rows, which):
        partial_sum = jnp.sum(sorted_rows)
        payload = jnp.concatenate(
            [
                sorted_rows.reshape(shard_count, per_peer, lane_count),
                jnp.broadcast_to(partial_sum, (shard_count, PAD, lane_count)),
            ],
            axis=1,
        )
        arrived_rows = lax.all_to_all(payload, "shard", 0, 0, tiled=True)
        total = jnp.sum(arrived_rows[:, per_peer, 0])
        rows = arrived_rows[:, :per_peer].reshape(block_count, lane_count)
        return segment_rows(rows, arrived[which], per_owner), total

    def fetch(owned_rows, which, partial=None):
        owned_rows = jnp.where(jnp.isfinite(owned_rows), owned_rows, 0.0)
        picked = gather_rows(owned_rows, arrived[which]).reshape(shard_count, per_peer, lane_count)
        if partial is not None:
            picked = jnp.concatenate(
                [picked, jnp.broadcast_to(partial, (shard_count, PAD, lane_count))], axis=1
            )
        back = lax.all_to_all(picked, "shard", 0, 0, tiled=True)
        if partial is None:
            return back.reshape(block_count, lane_count)
        rows = back[:, :per_peer].reshape(block_count, lane_count)
        return rows, jnp.sum(back[:, per_peer, 0])

    def route(owned_rows, mixing, partial=None):
        piece_rows = per_owner // clique_count
        pieces = owned_rows.reshape(clique_count, piece_rows, lane_count)
        if partial is not None:
            pieces = jnp.concatenate(
                [pieces, jnp.broadcast_to(partial, (clique_count, PAD, lane_count))], axis=1
            )
        combined = jnp.einsum(
            "oi,ixl->oxl",
            mixing,
            lax.all_to_all(pieces, "clique", split_axis=0, concat_axis=0, tiled=True),
            precision=lax.Precision.HIGHEST,
        )
        moved = lax.all_to_all(combined, "clique", split_axis=0, concat_axis=0, tiled=True)
        if partial is None:
            return moved.reshape(per_owner, lane_count)
        return moved[:, :piece_rows].reshape(per_owner, lane_count), moved[0, piece_rows, 0]

    clique_ids = jnp.arange(clique_count, dtype=jnp.int32)
    sel = [
        (parents[edge][:, None] == clique_ids[None, :]).astype(jnp.float32) for edge in (0, 1)
    ]
    t0, t1, t2 = tables[0, 0], tables[1, 0], tables[2, 0]

    t0_down0 = gather_rows(t0, order[2])
    down0_message, _ = send(t0_down0, 2)

    t2_up1 = gather_rows(t2, order[0])
    message, total = send(t2_up1, 0)
    scaled1 = message * (sep_states / total)
    incoming1 = jnp.exp(route(jnp.log(scaled1), sel[1].T))
    t1_down1 = gather_rows(t1, order[3]) * fetch(incoming1, 3)
    t1_up0 = gather_rows(t1_down1, moves[0])
    message, total = send(t1_up0, 1)
    scaled0 = message * (sep_states / total)
    incoming0 = jnp.exp(route(jnp.log(scaled0), sel[0].T))
    incoming0 = jnp.where(jnp.isfinite(incoming0), incoming0, 0.0)
    out0 = gather_rows(t0_down0 * fetch(incoming0, 2), position[2])
    fresh0 = down0_message * incoming0
    from_parent, partial = route(fresh0, sel[0], jnp.sum(fresh0))
    update0, total = fetch(from_parent / scaled0, 1, partial)
    t1_up0 = t1_up0 * (update0 * (sep_states / total))
    out1 = gather_rows(t1_up0, position[1])
    t1_down1 = gather_rows(t1_up0, moves[1])
    message, total = send(t1_down1, 3)
    fresh1 = message * (sep_states / total)
    update1 = route(fresh1, sel[1]) / scaled1
    t2_up1 = t2_up1 * fetch(update1, 0)
    out2 = gather_rows(t2_up1, position[0])
    return jnp.stack([out0, out1, out2])[:, None]


def solution(mesh):
    return jax.shard_map(
        shards,
        mesh=mesh,
        in_specs=(
            P(None, "clique", "shard", None),
            P(None, "clique", "shard"),
            P(None, "clique", "shard"),
            P(),
        ),
        out_specs=P(None, "clique", "shard", None),
        check_vma=False,
    )
```

```python
import jax
import jax.numpy as jnp
from jax import lax
from jax.sharding import PartitionSpec as P

SEPB = 4096
PAD = 8


def split_dot(one_hot, x, transposed=False):
    lanes = x.shape[-1]
    hi = lax.reduce_precision(x, exponent_bits=8, mantissa_bits=7)
    rest = x - hi
    mid = lax.reduce_precision(rest, exponent_bits=8, mantissa_bits=7)
    lo = rest - mid
    parts = jnp.concatenate([hi, mid, lo], axis=1).astype(jnp.bfloat16)
    contract = 0 if transposed else 1
    y = lax.dot_general(
        one_hot, parts, (((contract,), (0,)), ((), ())), preferred_element_type=jnp.float32
    )
    return (y[:, :lanes] + y[:, lanes : 2 * lanes]) + y[:, 2 * lanes :]


def one_hot_of(index, count):
    return (index[:, None] == jnp.arange(count, dtype=jnp.int32)[None, :]).astype(jnp.bfloat16)


def gather_rows(x, index):
    one_hot = (index[:, None] == jnp.arange(x.shape[0], dtype=jnp.int32)[None, :]).astype(
        jnp.bfloat16
    )
    return split_dot(one_hot, x)


def segment_rows(x, segment, count):
    one_hot = (jnp.arange(count, dtype=jnp.int32)[:, None] == segment[None, :]).astype(
        jnp.bfloat16
    )
    return split_dot(one_hot, x)


def shards(tables, up_map, down_map, parents):
    shard_count = lax.axis_size("shard")
    clique_count = lax.axis_size("clique")
    block_count = tables.shape[2]
    lane_count = tables.shape[3]
    per_owner = SEPB // shard_count
    per_peer = block_count // shard_count
    sep_states = float(SEPB * lane_count)

    lists = jnp.stack([up_map[1, 0], up_map[0, 0], down_map[0, 0], down_map[1, 0]])
    owner = lists // per_owner
    slot = lists % per_owner
    blocks = jnp.broadcast_to(jnp.arange(block_count, dtype=jnp.int32), lists.shape)
    _, sent_slots, order = lax.sort((owner, slot, blocks), dimension=1, num_keys=1, is_stable=True)
    arrived = lax.all_to_all(
        sent_slots.reshape(4, shard_count, per_peer), "shard", 1, 1, tiled=True
    ).reshape(4, block_count)
    sorting = [one_hot_of(order[which], block_count) for which in range(4)]
    down1_to_up0 = lax.dot_general(
        sorting[1], sorting[3], (((1,), (1,)), ((), ())), preferred_element_type=jnp.float32
    ).astype(jnp.bfloat16)

    def send(items):
        partial_sum = jnp.sum(items[0][0])
        chunks = [rows.reshape(shard_count, per_peer, lane_count) for rows, _ in items]
        chunks.append(jnp.broadcast_to(partial_sum, (shard_count, PAD, lane_count)))
        arrived_rows = lax.all_to_all(jnp.concatenate(chunks, axis=1), "shard", 0, 0, tiled=True)
        total = jnp.sum(arrived_rows[:, len(items) * per_peer, 0])
        messages = []
        for number, (_, which) in enumerate(items):
            rows = arrived_rows[:, number * per_peer : (number + 1) * per_peer]
            messages.append(
                segment_rows(rows.reshape(block_count, lane_count), arrived[which], per_owner)
            )
        return messages, total

    def fetch(items, partial=None):
        chunks = []
        for owned_rows, which in items:
            owned_rows = jnp.where(jnp.isfinite(owned_rows), owned_rows, 0.0)
            picked = gather_rows(owned_rows, arrived[which])
            chunks.append(picked.reshape(shard_count, per_peer, lane_count))
        if partial is not None:
            chunks.append(jnp.broadcast_to(partial, (shard_count, PAD, lane_count)))
        back = lax.all_to_all(jnp.concatenate(chunks, axis=1), "shard", 0, 0, tiled=True)
        rows = [
            back[:, number * per_peer : (number + 1) * per_peer].reshape(block_count, lane_count)
            for number in range(len(items))
        ]
        if partial is None:
            return rows, None
        return rows, jnp.sum(back[:, len(items) * per_peer, 0])

    def route(owned_rows, mixing, partial=None):
        piece_rows = per_owner // clique_count
        pieces = owned_rows.reshape(clique_count, piece_rows, lane_count)
        if partial is not None:
            pieces = jnp.concatenate(
                [pieces, jnp.broadcast_to(partial, (clique_count, PAD, lane_count))], axis=1
            )
        combined = jnp.einsum(
            "oi,ixl->oxl",
            mixing,
            lax.all_to_all(pieces, "clique", split_axis=0, concat_axis=0, tiled=True),
            precision=lax.Precision.HIGHEST,
        )
        moved = lax.all_to_all(combined, "clique", split_axis=0, concat_axis=0, tiled=True)
        if partial is None:
            return moved.reshape(per_owner, lane_count)
        return moved[:, :piece_rows].reshape(per_owner, lane_count), moved[0, piece_rows, 0]

    clique_ids = jnp.arange(clique_count, dtype=jnp.int32)
    sel = [
        (parents[edge][:, None] == clique_ids[None, :]).astype(jnp.float32) for edge in (0, 1)
    ]
    t0, t1, t2 = tables[0, 0], tables[1, 0], tables[2, 0]

    t2_up1 = split_dot(sorting[0], t2)
    t0_down0 = split_dot(sorting[2], t0)
    (message, down0_message), total = send([(t2_up1, 0), (t0_down0, 2)])
    scaled1 = message * (sep_states / total)
    incoming1 = jnp.exp(route(jnp.log(scaled1), sel[1].T))
    (picked,), _ = fetch([(incoming1, 3)])
    t1_down1 = split_dot(sorting[3], t1) * picked
    t1_up0 = split_dot(down1_to_up0, t1_down1)
    (message,), total = send([(t1_up0, 1)])
    scaled0 = message * (sep_states / total)
    incoming0 = jnp.exp(route(jnp.log(scaled0), sel[0].T))
    incoming0 = jnp.where(jnp.isfinite(incoming0), incoming0, 0.0)
    fresh0 = down0_message * incoming0
    from_parent, partial = route(fresh0, sel[0], jnp.sum(fresh0))
    (picked, update0), total = fetch([(incoming0, 2), (from_parent / scaled0, 1)], partial)
    out0 = split_dot(sorting[2], t0_down0 * picked, transposed=True)
    t1_up0 = t1_up0 * (update0 * (sep_states / total))
    out1 = split_dot(sorting[1], t1_up0, transposed=True)
    t1_down1 = split_dot(down1_to_up0, t1_up0, transposed=True)
    (message,), total = send([(t1_down1, 3)])
    fresh1 = message * (sep_states / total)
    update1 = route(fresh1, sel[1]) / scaled1
    (picked,), _ = fetch([(update1, 0)])
    out2 = split_dot(sorting[0], t2_up1 * picked, transposed=True)
    return jnp.stack([out0, out1, out2])[:, None]


def solution(mesh):
    return jax.shard_map(
        shards,
        mesh=mesh,
        in_specs=(
            P(None, "clique", "shard", None),
            P(None, "clique", "shard"),
            P(None, "clique", "shard"),
            P(),
        ),
        out_specs=P(None, "clique", "shard", None),
        check_vma=False,
    )
```

```python
import jax
import jax.numpy as jnp
from jax import lax
from jax.sharding import PartitionSpec as P

SEPB = 4096
PAD = 8


def split_dot(one_hot, x, transposed=False):
    lanes = x.shape[-1]
    hi = lax.reduce_precision(x, exponent_bits=8, mantissa_bits=7)
    rest = x - hi
    mid = lax.reduce_precision(rest, exponent_bits=8, mantissa_bits=7)
    lo = rest - mid
    parts = jnp.concatenate([hi, mid, lo], axis=1).astype(jnp.bfloat16)
    contract = 0 if transposed else 1
    y = lax.dot_general(
        one_hot, parts, (((contract,), (0,)), ((), ())), preferred_element_type=jnp.float32
    )
    return (y[:, :lanes] + y[:, lanes : 2 * lanes]) + y[:, 2 * lanes :]


def one_hot_of(index, count):
    return (index[:, None] == jnp.arange(count, dtype=jnp.int32)[None, :]).astype(jnp.bfloat16)


def gather_rows(x, index):
    one_hot = (index[:, None] == jnp.arange(x.shape[0], dtype=jnp.int32)[None, :]).astype(
        jnp.bfloat16
    )
    return split_dot(one_hot, x)


def segment_rows(x, segment, count):
    one_hot = (jnp.arange(count, dtype=jnp.int32)[:, None] == segment[None, :]).astype(
        jnp.bfloat16
    )
    return split_dot(one_hot, x)


def shards(tables, up_map, down_map, parents):
    shard_count = lax.axis_size("shard")
    clique_count = lax.axis_size("clique")
    block_count = tables.shape[2]
    lane_count = tables.shape[3]
    per_owner = SEPB // shard_count
    per_peer = block_count // shard_count
    sep_states = float(SEPB * lane_count)

    lists = jnp.stack([up_map[1, 0], up_map[0, 0], down_map[0, 0], down_map[1, 0]])
    owner = lists // per_owner
    slot = lists % per_owner
    blocks = jnp.broadcast_to(jnp.arange(block_count, dtype=jnp.int32), lists.shape)
    _, sent_slots, order = lax.sort((owner, slot, blocks), dimension=1, num_keys=1, is_stable=True)
    sorting = [one_hot_of(order[which], block_count) for which in range(4)]
    down1_to_up0 = lax.dot_general(
        sorting[1], sorting[3], (((1,), (1,)), ((), ())), preferred_element_type=jnp.float32
    ).astype(jnp.bfloat16)
    slot_rows = (4 * per_peer) // lane_count
    slot_chunk = (
        sent_slots.reshape(4, shard_count, per_peer)
        .transpose(1, 0, 2)
        .reshape(shard_count, slot_rows, lane_count)
        .astype(jnp.float32)
    )
    arrived = [None] * 4
    piece_rows = per_owner // clique_count

    def send(items, with_slots=False):
        partial_sum = jnp.sum(items[0][0])
        chunks = [rows.reshape(shard_count, per_peer, lane_count) for rows, _ in items]
        chunks.append(jnp.broadcast_to(partial_sum, (shard_count, PAD, lane_count)))
        if with_slots:
            chunks.append(slot_chunk)
        arrived_rows = lax.all_to_all(jnp.concatenate(chunks, axis=1), "shard", 0, 0, tiled=True)
        head = len(items) * per_peer
        total = jnp.sum(arrived_rows[:, head, 0])
        if with_slots:
            got = arrived_rows[:, head + PAD :].reshape(shard_count, 4, per_peer)
            got = got.transpose(1, 0, 2).reshape(4, block_count).astype(jnp.int32)
            for which in range(4):
                arrived[which] = got[which]
        messages = []
        for number, (_, which) in enumerate(items):
            rows = arrived_rows[:, number * per_peer : (number + 1) * per_peer]
            messages.append(
                segment_rows(rows.reshape(block_count, lane_count), arrived[which], per_owner)
            )
        return messages, total

    def fetch(items, partial=None):
        chunks = []
        for owned_rows, which in items:
            owned_rows = jnp.where(jnp.isfinite(owned_rows), owned_rows, 0.0)
            picked = gather_rows(owned_rows, arrived[which])
            chunks.append(picked.reshape(shard_count, per_peer, lane_count))
        if partial is not None:
            chunks.append(jnp.broadcast_to(partial, (shard_count, PAD, lane_count)))
        back = lax.all_to_all(jnp.concatenate(chunks, axis=1), "shard", 0, 0, tiled=True)
        rows = [
            back[:, number * per_peer : (number + 1) * per_peer].reshape(block_count, lane_count)
            for number in range(len(items))
        ]
        if partial is None:
            return rows, None
        return rows, jnp.sum(back[:, len(items) * per_peer, 0])

    def to_middle(arrays):
        pieces = [a.reshape(clique_count, piece_rows, lane_count) for a in arrays]
        got = lax.all_to_all(jnp.concatenate(pieces, axis=1), "clique", 0, 0, tiled=True)
        return [got[:, n * piece_rows : (n + 1) * piece_rows] for n in range(len(arrays))]

    def from_middle(arrays, partial=None):
        chunks = list(arrays)
        if partial is not None:
            chunks.append(jnp.broadcast_to(partial[:, None, None], (clique_count, PAD, lane_count)))
        got = lax.all_to_all(jnp.concatenate(chunks, axis=1), "clique", 0, 0, tiled=True)
        outs = [
            got[:, n * piece_rows : (n + 1) * piece_rows].reshape(per_owner, lane_count)
            for n in range(len(arrays))
        ]
        if partial is None:
            return outs, None
        return outs, jnp.sum(got[:, len(arrays) * piece_rows, 0])

    def mix(mixing, pieces):
        return jnp.einsum("oi,ixl->oxl", mixing, pieces, precision=lax.Precision.HIGHEST)

    clique_ids = jnp.arange(clique_count, dtype=jnp.int32)
    sel = [
        (parents[edge][:, None] == clique_ids[None, :]).astype(jnp.float32) for edge in (0, 1)
    ]
    t0, t1, t2 = tables[0, 0], tables[1, 0], tables[2, 0]

    t2_up1 = split_dot(sorting[0], t2)
    t0_down0 = split_dot(sorting[2], t0)
    (message, down0_message), total = send([(t2_up1, 0), (t0_down0, 2)], with_slots=True)
    scaled1 = message * (sep_states / total)
    scaled1_mid, down0_mid = to_middle([scaled1, down0_message])
    (incoming1,), _ = from_middle([jnp.exp(mix(sel[1].T, jnp.log(scaled1_mid)))])
    (picked,), _ = fetch([(incoming1, 3)])
    t1_down1 = split_dot(sorting[3], t1) * picked
    t1_up0 = split_dot(down1_to_up0, t1_down1)
    (message,), total = send([(t1_up0, 1)])
    scaled0 = message * (sep_states / total)
    (scaled0_mid,) = to_middle([scaled0])
    incoming0_mid = jnp.exp(mix(sel[0].T, jnp.log(scaled0_mid)))
    incoming0_mid = jnp.where(jnp.isfinite(incoming0_mid), incoming0_mid, 0.0)
    fresh0_mid = down0_mid * incoming0_mid
    partial = jnp.dot(sel[0], jnp.sum(fresh0_mid, axis=(1, 2)), precision=lax.Precision.HIGHEST)
    update0_mid = mix(sel[0], fresh0_mid) / scaled0_mid
    (update0, incoming0), range_total = from_middle([update0_mid, incoming0_mid], partial)
    (picked, update0), total = fetch([(incoming0, 2), (update0, 1)], range_total)
    out0 = split_dot(sorting[2], t0_down0 * picked, transposed=True)
    t1_up0 = t1_up0 * (update0 * (sep_states / total))
    out1 = split_dot(sorting[1], t1_up0, transposed=True)
    t1_down1 = split_dot(down1_to_up0, t1_up0, transposed=True)
    (message,), total = send([(t1_down1, 3)])
    fresh1 = message * (sep_states / total)
    (fresh1_mid,) = to_middle([fresh1])
    (update1,), _ = from_middle([mix(sel[1], fresh1_mid) / scaled1_mid])
    (picked,), _ = fetch([(update1, 0)])
    out2 = split_dot(sorting[0], t2_up1 * picked, transposed=True)
    return jnp.stack([out0, out1, out2])[:, None]


def solution(mesh):
    return jax.shard_map(
        shards,
        mesh=mesh,
        in_specs=(
            P(None, "clique", "shard", None),
            P(None, "clique", "shard"),
            P(None, "clique", "shard"),
            P(),
        ),
        out_specs=P(None, "clique", "shard", None),
        check_vma=False,
    )
```

```python
import jax
import jax.numpy as jnp
from jax import lax
from jax.sharding import PartitionSpec as P

SEPB = 4096
PAD = 8


def split_dot(one_hot, x, transposed=False):
    lanes = x.shape[-1]
    hi = lax.reduce_precision(x, exponent_bits=8, mantissa_bits=7)
    rest = x - hi
    mid = lax.reduce_precision(rest, exponent_bits=8, mantissa_bits=7)
    lo = rest - mid
    parts = jnp.concatenate([hi, mid, lo], axis=1).astype(jnp.bfloat16)
    contract = 0 if transposed else 1
    y = lax.dot_general(
        one_hot, parts, (((contract,), (0,)), ((), ())), preferred_element_type=jnp.float32
    )
    return (y[:, :lanes] + y[:, lanes : 2 * lanes]) + y[:, 2 * lanes :]


def one_hot_of(index, count):
    return (index[:, None] == jnp.arange(count, dtype=jnp.int32)[None, :]).astype(jnp.bfloat16)


def gather_rows(x, index):
    one_hot = (index[:, None] == jnp.arange(x.shape[0], dtype=jnp.int32)[None, :]).astype(
        jnp.bfloat16
    )
    return split_dot(one_hot, x)


def segment_rows(x, segment, count):
    one_hot = (jnp.arange(count, dtype=jnp.int32)[:, None] == segment[None, :]).astype(
        jnp.bfloat16
    )
    return split_dot(one_hot, x)


def permute_all_to_all(chunks, axis):
    count = chunks.shape[0]
    me = lax.axis_index(axis)
    got = [lax.dynamic_index_in_dim(chunks, me, 0, keepdims=False)]
    for shift in range(1, count):
        piece = lax.dynamic_index_in_dim(chunks, (me + shift) % count, 0, keepdims=False)
        pairs = [(source, (source + shift) % count) for source in range(count)]
        got.append(lax.ppermute(piece, axis, pairs))
    stacked = jnp.stack(got)
    sources = (me - jnp.arange(count, dtype=jnp.int32)) % count
    return jnp.take(stacked, sources, axis=0)


def shards(tables, up_map, down_map, parents):
    shard_count = lax.axis_size("shard")
    clique_count = lax.axis_size("clique")
    block_count = tables.shape[2]
    lane_count = tables.shape[3]
    per_owner = SEPB // shard_count
    per_peer = block_count // shard_count
    sep_states = float(SEPB * lane_count)

    lists = jnp.stack([up_map[1, 0], up_map[0, 0], down_map[0, 0], down_map[1, 0]])
    owner = lists // per_owner
    slot = lists % per_owner
    blocks = jnp.broadcast_to(jnp.arange(block_count, dtype=jnp.int32), lists.shape)
    _, sent_slots, order = lax.sort((owner, slot, blocks), dimension=1, num_keys=1, is_stable=True)
    sorting = [one_hot_of(order[which], block_count) for which in range(4)]
    down1_to_up0 = lax.dot_general(
        sorting[1], sorting[3], (((1,), (1,)), ((), ())), preferred_element_type=jnp.float32
    ).astype(jnp.bfloat16)
    slot_rows = (4 * per_peer) // lane_count
    slot_chunk = (
        sent_slots.reshape(4, shard_count, per_peer)
        .transpose(1, 0, 2)
        .reshape(shard_count, slot_rows, lane_count)
        .astype(jnp.float32)
    )
    arrived = [None] * 4
    piece_rows = per_owner // clique_count

    def send(items, with_slots=False):
        partial_sum = jnp.sum(items[0][0])
        chunks = [rows.reshape(shard_count, per_peer, lane_count) for rows, _ in items]
        chunks.append(jnp.broadcast_to(partial_sum, (shard_count, PAD, lane_count)))
        if with_slots:
            chunks.append(slot_chunk)
        arrived_rows = lax.all_to_all(jnp.concatenate(chunks, axis=1), "shard", 0, 0, tiled=True)
        head = len(items) * per_peer
        total = jnp.sum(arrived_rows[:, head, 0])
        if with_slots:
            got = arrived_rows[:, head + PAD :].reshape(shard_count, 4, per_peer)
            got = got.transpose(1, 0, 2).reshape(4, block_count).astype(jnp.int32)
            for which in range(4):
                arrived[which] = got[which]
        messages = []
        for number, (_, which) in enumerate(items):
            rows = arrived_rows[:, number * per_peer : (number + 1) * per_peer]
            messages.append(
                segment_rows(rows.reshape(block_count, lane_count), arrived[which], per_owner)
            )
        return messages, total

    def fetch(items, partial=None):
        chunks = []
        for owned_rows, which in items:
            owned_rows = jnp.where(jnp.isfinite(owned_rows), owned_rows, 0.0)
            picked = gather_rows(owned_rows, arrived[which])
            chunks.append(picked.reshape(shard_count, per_peer, lane_count))
        if partial is not None:
            chunks.append(jnp.broadcast_to(partial, (shard_count, PAD, lane_count)))
        back = lax.all_to_all(jnp.concatenate(chunks, axis=1), "shard", 0, 0, tiled=True)
        rows = [
            back[:, number * per_peer : (number + 1) * per_peer].reshape(block_count, lane_count)
            for number in range(len(items))
        ]
        if partial is None:
            return rows, None
        return rows, jnp.sum(back[:, len(items) * per_peer, 0])

    def to_middle(arrays):
        pieces = [a.reshape(clique_count, piece_rows, lane_count) for a in arrays]
        got = lax.all_to_all(jnp.concatenate(pieces, axis=1), "clique", 0, 0, tiled=True)
        return [got[:, n * piece_rows : (n + 1) * piece_rows] for n in range(len(arrays))]

    def from_middle(arrays, partial=None):
        chunks = list(arrays)
        if partial is not None:
            chunks.append(jnp.broadcast_to(partial[:, None, None], (clique_count, PAD, lane_count)))
        got = lax.all_to_all(jnp.concatenate(chunks, axis=1), "clique", 0, 0, tiled=True)
        outs = [
            got[:, n * piece_rows : (n + 1) * piece_rows].reshape(per_owner, lane_count)
            for n in range(len(arrays))
        ]
        if partial is None:
            return outs, None
        return outs, jnp.sum(got[:, len(arrays) * piece_rows, 0])

    def mix(mixing, pieces):
        return jnp.einsum("oi,ixl->oxl", mixing, pieces, precision=lax.Precision.HIGHEST)

    clique_ids = jnp.arange(clique_count, dtype=jnp.int32)
    sel = [
        (parents[edge][:, None] == clique_ids[None, :]).astype(jnp.float32) for edge in (0, 1)
    ]
    t0, t1, t2 = tables[0, 0], tables[1, 0], tables[2, 0]

    t2_up1 = split_dot(sorting[0], t2)
    (message,), total = send([(t2_up1, 0)], with_slots=True)
    scaled1 = message * (sep_states / total)
    (scaled1_mid,) = to_middle([scaled1])
    t0_down0 = split_dot(sorting[2], t0)
    rows = permute_all_to_all(t0_down0.reshape(shard_count, per_peer, lane_count), "shard")
    down0_message = segment_rows(rows.reshape(block_count, lane_count), arrived[2], per_owner)
    down0_mid = permute_all_to_all(
        down0_message.reshape(clique_count, piece_rows, lane_count), "clique"
    )
    (incoming1,), _ = from_middle([jnp.exp(mix(sel[1].T, jnp.log(scaled1_mid)))])
    (picked,), _ = fetch([(incoming1, 3)])
    t1_down1 = split_dot(sorting[3], t1) * picked
    t1_up0 = split_dot(down1_to_up0, t1_down1)
    (message,), total = send([(t1_up0, 1)])
    scaled0 = message * (sep_states / total)
    (scaled0_mid,) = to_middle([scaled0])
    incoming0_mid = jnp.exp(mix(sel[0].T, jnp.log(scaled0_mid)))
    incoming0_mid = jnp.where(jnp.isfinite(incoming0_mid), incoming0_mid, 0.0)
    fresh0_mid = down0_mid * incoming0_mid
    partial = jnp.dot(sel[0], jnp.sum(fresh0_mid, axis=(1, 2)), precision=lax.Precision.HIGHEST)
    update0_mid = mix(sel[0], fresh0_mid) / scaled0_mid
    (update0,), range_total = from_middle([update0_mid], partial)
    (update0,), total = fetch([(update0, 1)], range_total)
    t1_up0 = t1_up0 * (update0 * (sep_states / total))
    out1 = split_dot(sorting[1], t1_up0, transposed=True)
    incoming0 = permute_all_to_all(incoming0_mid, "clique").reshape(per_owner, lane_count)
    picked = gather_rows(incoming0, arrived[2]).reshape(shard_count, per_peer, lane_count)
    picked = permute_all_to_all(picked, "shard").reshape(block_count, lane_count)
    out0 = split_dot(sorting[2], t0_down0 * picked, transposed=True)
    t1_down1 = split_dot(down1_to_up0, t1_up0, transposed=True)
    (message,), total = send([(t1_down1, 3)])
    fresh1 = message * (sep_states / total)
    (fresh1_mid,) = to_middle([fresh1])
    (update1,), _ = from_middle([mix(sel[1], fresh1_mid) / scaled1_mid])
    (picked,), _ = fetch([(update1, 0)])
    out2 = split_dot(sorting[0], t2_up1 * picked, transposed=True)
    return jnp.stack([out0, out1, out2])[:, None]


def solution(mesh):
    return jax.shard_map(
        shards,
        mesh=mesh,
        in_specs=(
            P(None, "clique", "shard", None),
            P(None, "clique", "shard"),
            P(None, "clique", "shard"),
            P(),
        ),
        out_specs=P(None, "clique", "shard", None),
        check_vma=False,
    )
```

```python
import jax
import jax.numpy as jnp
from jax import lax
from jax.sharding import PartitionSpec as P

SEPB = 4096
PAD = 8


def split_dot(one_hot, x, transposed=False):
    lanes = x.shape[-1]
    hi = lax.reduce_precision(x, exponent_bits=8, mantissa_bits=7)
    lo = x - hi
    parts = jnp.concatenate([hi, lo], axis=1).astype(jnp.bfloat16)
    contract = 0 if transposed else 1
    y = lax.dot_general(
        one_hot, parts, (((contract,), (0,)), ((), ())), preferred_element_type=jnp.float32
    )
    return y[:, :lanes] + y[:, lanes:]


def one_hot_of(index, count):
    return (index[:, None] == jnp.arange(count, dtype=jnp.int32)[None, :]).astype(jnp.bfloat16)


def gather_rows(x, index):
    one_hot = (index[:, None] == jnp.arange(x.shape[0], dtype=jnp.int32)[None, :]).astype(
        jnp.bfloat16
    )
    return split_dot(one_hot, x)


def segment_rows(x, segment, count):
    one_hot = (jnp.arange(count, dtype=jnp.int32)[:, None] == segment[None, :]).astype(
        jnp.bfloat16
    )
    return split_dot(one_hot, x)


def shards(tables, up_map, down_map, parents):
    shard_count = lax.axis_size("shard")
    clique_count = lax.axis_size("clique")
    block_count = tables.shape[2]
    lane_count = tables.shape[3]
    per_owner = SEPB // shard_count
    per_peer = block_count // shard_count
    sep_states = float(SEPB * lane_count)

    lists = jnp.stack([up_map[1, 0], up_map[0, 0], down_map[0, 0], down_map[1, 0]])
    owner = lists // per_owner
    slot = lists % per_owner
    blocks = jnp.broadcast_to(jnp.arange(block_count, dtype=jnp.int32), lists.shape)
    _, sent_slots, order = lax.sort((owner, slot, blocks), dimension=1, num_keys=1, is_stable=True)
    sorting = [one_hot_of(order[which], block_count) for which in range(4)]
    down1_to_up0 = lax.dot_general(
        sorting[1], sorting[3], (((1,), (1,)), ((), ())), preferred_element_type=jnp.float32
    ).astype(jnp.bfloat16)
    slot_rows = (4 * per_peer) // lane_count
    slot_chunk = (
        sent_slots.reshape(4, shard_count, per_peer)
        .transpose(1, 0, 2)
        .reshape(shard_count, slot_rows, lane_count)
        .astype(jnp.float32)
    )
    arrived = [None] * 4
    piece_rows = per_owner // clique_count

    def send(items, with_slots=False):
        partial_sum = jnp.sum(items[0][0])
        chunks = [rows.reshape(shard_count, per_peer, lane_count) for rows, _ in items]
        chunks.append(jnp.broadcast_to(partial_sum, (shard_count, PAD, lane_count)))
        if with_slots:
            chunks.append(slot_chunk)
        arrived_rows = lax.all_to_all(jnp.concatenate(chunks, axis=1), "shard", 0, 0, tiled=True)
        head = len(items) * per_peer
        total = jnp.sum(arrived_rows[:, head, 0])
        if with_slots:
            got = arrived_rows[:, head + PAD :].reshape(shard_count, 4, per_peer)
            got = got.transpose(1, 0, 2).reshape(4, block_count).astype(jnp.int32)
            for which in range(4):
                arrived[which] = got[which]
        messages = []
        for number, (_, which) in enumerate(items):
            rows = arrived_rows[:, number * per_peer : (number + 1) * per_peer]
            messages.append(
                segment_rows(rows.reshape(block_count, lane_count), arrived[which], per_owner)
            )
        return messages, total

    def fetch(items, partial=None):
        chunks = []
        for owned_rows, which in items:
            owned_rows = jnp.where(jnp.isfinite(owned_rows), owned_rows, 0.0)
            picked = gather_rows(owned_rows, arrived[which])
            chunks.append(picked.reshape(shard_count, per_peer, lane_count))
        if partial is not None:
            chunks.append(jnp.broadcast_to(partial, (shard_count, PAD, lane_count)))
        back = lax.all_to_all(jnp.concatenate(chunks, axis=1), "shard", 0, 0, tiled=True)
        rows = [
            back[:, number * per_peer : (number + 1) * per_peer].reshape(block_count, lane_count)
            for number in range(len(items))
        ]
        if partial is None:
            return rows, None
        return rows, jnp.sum(back[:, len(items) * per_peer, 0])

    def to_middle(arrays):
        pieces = [a.reshape(clique_count, piece_rows, lane_count) for a in arrays]
        got = lax.all_to_all(jnp.concatenate(pieces, axis=1), "clique", 0, 0, tiled=True)
        return [got[:, n * piece_rows : (n + 1) * piece_rows] for n in range(len(arrays))]

    def from_middle(arrays, partial=None):
        chunks = list(arrays)
        if partial is not None:
            chunks.append(jnp.broadcast_to(partial[:, None, None], (clique_count, PAD, lane_count)))
        got = lax.all_to_all(jnp.concatenate(chunks, axis=1), "clique", 0, 0, tiled=True)
        outs = [
            got[:, n * piece_rows : (n + 1) * piece_rows].reshape(per_owner, lane_count)
            for n in range(len(arrays))
        ]
        if partial is None:
            return outs, None
        return outs, jnp.sum(got[:, len(arrays) * piece_rows, 0])

    def mix(mixing, pieces):
        return jnp.einsum("oi,ixl->oxl", mixing, pieces, precision=lax.Precision.HIGHEST)

    clique_ids = jnp.arange(clique_count, dtype=jnp.int32)
    sel = [
        (parents[edge][:, None] == clique_ids[None, :]).astype(jnp.float32) for edge in (0, 1)
    ]
    t0, t1, t2 = tables[0, 0], tables[1, 0], tables[2, 0]

    t2_up1 = split_dot(sorting[0], t2)
    t0_down0 = split_dot(sorting[2], t0)
    (message, down0_message), total = send([(t2_up1, 0), (t0_down0, 2)], with_slots=True)
    scaled1 = message * (sep_states / total)
    scaled1_mid, down0_mid = to_middle([scaled1, down0_message])
    (incoming1,), _ = from_middle([jnp.exp(mix(sel[1].T, jnp.log(scaled1_mid)))])
    (picked,), _ = fetch([(incoming1, 3)])
    t1_down1 = split_dot(sorting[3], t1) * picked
    t1_up0 = split_dot(down1_to_up0, t1_down1)
    (message,), total = send([(t1_up0, 1)])
    scaled0 = message * (sep_states / total)
    (scaled0_mid,) = to_middle([scaled0])
    incoming0_mid = jnp.exp(mix(sel[0].T, jnp.log(scaled0_mid)))
    incoming0_mid = jnp.where(jnp.isfinite(incoming0_mid), incoming0_mid, 0.0)
    fresh0_mid = down0_mid * incoming0_mid
    partial = jnp.dot(sel[0], jnp.sum(fresh0_mid, axis=(1, 2)), precision=lax.Precision.HIGHEST)
    update0_mid = mix(sel[0], fresh0_mid) / scaled0_mid
    (update0, incoming0), range_total = from_middle([update0_mid, incoming0_mid], partial)
    (picked, update0), total = fetch([(incoming0, 2), (update0, 1)], range_total)
    out0 = split_dot(sorting[2], t0_down0 * picked, transposed=True)
    t1_up0 = t1_up0 * (update0 * (sep_states / total))
    out1 = split_dot(sorting[1], t1_up0, transposed=True)
    t1_down1 = split_dot(down1_to_up0, t1_up0, transposed=True)
    (message,), total = send([(t1_down1, 3)])
    fresh1 = message * (sep_states / total)
    (fresh1_mid,) = to_middle([fresh1])
    (update1,), _ = from_middle([mix(sel[1], fresh1_mid) / scaled1_mid])
    (picked,), _ = fetch([(update1, 0)])
    out2 = split_dot(sorting[0], t2_up1 * picked, transposed=True)
    return jnp.stack([out0, out1, out2])[:, None]


def solution(mesh):
    return jax.shard_map(
        shards,
        mesh=mesh,
        in_specs=(
            P(None, "clique", "shard", None),
            P(None, "clique", "shard"),
            P(None, "clique", "shard"),
            P(),
        ),
        out_specs=P(None, "clique", "shard", None),
        check_vma=False,
    )
```

```python
import jax
import jax.numpy as jnp
from jax import lax
from jax.sharding import PartitionSpec as P

SEPB = 4096
PAD = 8


def split_dot(one_hot, x, transposed=False):
    lanes = x.shape[-1]
    hi = lax.reduce_precision(x, exponent_bits=8, mantissa_bits=7)
    lo = x - hi
    parts = jnp.concatenate([hi, lo], axis=1).astype(jnp.bfloat16)
    contract = 0 if transposed else 1
    y = lax.dot_general(
        one_hot, parts, (((contract,), (0,)), ((), ())), preferred_element_type=jnp.float32
    )
    return y[:, :lanes] + y[:, lanes:]


def one_hot_of(index, count):
    return (index[:, None] == jnp.arange(count, dtype=jnp.int32)[None, :]).astype(jnp.bfloat16)


def gather_rows(x, index):
    one_hot = (index[:, None] == jnp.arange(x.shape[0], dtype=jnp.int32)[None, :]).astype(
        jnp.bfloat16
    )
    return split_dot(one_hot, x)


def segment_rows(x, segment, count):
    one_hot = (jnp.arange(count, dtype=jnp.int32)[:, None] == segment[None, :]).astype(
        jnp.bfloat16
    )
    return split_dot(one_hot, x)


def shards(tables, up_map, down_map, parents):
    shard_count = lax.axis_size("shard")
    clique_count = lax.axis_size("clique")
    block_count = tables.shape[2]
    lane_count = tables.shape[3]
    per_owner = SEPB // shard_count
    per_peer = block_count // shard_count
    sep_states = float(SEPB * lane_count)

    lists = jnp.stack([up_map[1, 0], up_map[0, 0], down_map[0, 0], down_map[1, 0]])
    owner = lists // per_owner
    slot = lists % per_owner
    owned = (owner[:, :, None] == jnp.arange(shard_count, dtype=jnp.int32)).astype(jnp.bfloat16)
    earlier = (
        jnp.arange(block_count, dtype=jnp.int32)[:, None]
        >= jnp.arange(block_count, dtype=jnp.int32)[None, :]
    ).astype(jnp.bfloat16)
    counts = jnp.einsum("bc,lco->lbo", earlier, owned, preferred_element_type=jnp.float32)
    rank = jnp.sum(counts * owned.astype(jnp.float32), axis=2).astype(jnp.int32) - 1
    position = owner * per_peer + rank
    sorting = [
        (jnp.arange(block_count, dtype=jnp.int32)[:, None] == position[which][None, :]).astype(
            jnp.bfloat16
        )
        for which in range(4)
    ]
    halves = jnp.stack([slot // 32, slot % 32], axis=2).astype(jnp.bfloat16)
    sent_halves = jnp.einsum(
        "lib,lbh->lih", jnp.stack(sorting), halves, preferred_element_type=jnp.float32
    )
    sent_slots = (sent_halves[:, :, 0] * 32 + sent_halves[:, :, 1]).astype(jnp.int32)
    down1_to_up0 = lax.dot_general(
        sorting[1], sorting[3], (((1,), (1,)), ((), ())), preferred_element_type=jnp.float32
    ).astype(jnp.bfloat16)
    slot_rows = (4 * per_peer) // lane_count
    slot_chunk = (
        sent_slots.reshape(4, shard_count, per_peer)
        .transpose(1, 0, 2)
        .reshape(shard_count, slot_rows, lane_count)
        .astype(jnp.float32)
    )
    arrived = [None] * 4
    piece_rows = per_owner // clique_count

    def send(items, with_slots=False):
        partial_sum = jnp.sum(items[0][0])
        chunks = [rows.reshape(shard_count, per_peer, lane_count) for rows, _ in items]
        chunks.append(jnp.broadcast_to(partial_sum, (shard_count, PAD, lane_count)))
        if with_slots:
            chunks.append(slot_chunk)
        arrived_rows = lax.all_to_all(jnp.concatenate(chunks, axis=1), "shard", 0, 0, tiled=True)
        head = len(items) * per_peer
        total = jnp.sum(arrived_rows[:, head, 0])
        if with_slots:
            got = arrived_rows[:, head + PAD :].reshape(shard_count, 4, per_peer)
            got = got.transpose(1, 0, 2).reshape(4, block_count).astype(jnp.int32)
            for which in range(4):
                arrived[which] = got[which]
        messages = []
        for number, (_, which) in enumerate(items):
            rows = arrived_rows[:, number * per_peer : (number + 1) * per_peer]
            messages.append(
                segment_rows(rows.reshape(block_count, lane_count), arrived[which], per_owner)
            )
        return messages, total

    def fetch(items, partial=None):
        chunks = []
        for owned_rows, which in items:
            owned_rows = jnp.where(jnp.isfinite(owned_rows), owned_rows, 0.0)
            picked = gather_rows(owned_rows, arrived[which])
            chunks.append(picked.reshape(shard_count, per_peer, lane_count))
        if partial is not None:
            chunks.append(jnp.broadcast_to(partial, (shard_count, PAD, lane_count)))
        back = lax.all_to_all(jnp.concatenate(chunks, axis=1), "shard", 0, 0, tiled=True)
        rows = [
            back[:, number * per_peer : (number + 1) * per_peer].reshape(block_count, lane_count)
            for number in range(len(items))
        ]
        if partial is None:
            return rows, None
        return rows, jnp.sum(back[:, len(items) * per_peer, 0])

    def to_middle(arrays):
        pieces = [a.reshape(clique_count, piece_rows, lane_count) for a in arrays]
        got = lax.all_to_all(jnp.concatenate(pieces, axis=1), "clique", 0, 0, tiled=True)
        return [got[:, n * piece_rows : (n + 1) * piece_rows] for n in range(len(arrays))]

    def from_middle(arrays, partial=None):
        chunks = list(arrays)
        if partial is not None:
            chunks.append(jnp.broadcast_to(partial[:, None, None], (clique_count, PAD, lane_count)))
        got = lax.all_to_all(jnp.concatenate(chunks, axis=1), "clique", 0, 0, tiled=True)
        outs = [
            got[:, n * piece_rows : (n + 1) * piece_rows].reshape(per_owner, lane_count)
            for n in range(len(arrays))
        ]
        if partial is None:
            return outs, None
        return outs, jnp.sum(got[:, len(arrays) * piece_rows, 0])

    def mix(mixing, pieces):
        return jnp.einsum("oi,ixl->oxl", mixing, pieces, precision=lax.Precision.HIGHEST)

    clique_ids = jnp.arange(clique_count, dtype=jnp.int32)
    sel = [
        (parents[edge][:, None] == clique_ids[None, :]).astype(jnp.float32) for edge in (0, 1)
    ]
    t0, t1, t2 = tables[0, 0], tables[1, 0], tables[2, 0]

    t2_up1 = split_dot(sorting[0], t2)
    t0_down0 = split_dot(sorting[2], t0)
    (message, down0_message), total = send([(t2_up1, 0), (t0_down0, 2)], with_slots=True)
    scaled1 = message * (sep_states / total)
    scaled1_mid, down0_mid = to_middle([scaled1, down0_message])
    (incoming1,), _ = from_middle([jnp.exp(mix(sel[1].T, jnp.log(scaled1_mid)))])
    (picked,), _ = fetch([(incoming1, 3)])
    t1_down1 = split_dot(sorting[3], t1) * picked
    t1_up0 = split_dot(down1_to_up0, t1_down1)
    (message,), total = send([(t1_up0, 1)])
    scaled0 = message * (sep_states / total)
    (scaled0_mid,) = to_middle([scaled0])
    incoming0_mid = jnp.exp(mix(sel[0].T, jnp.log(scaled0_mid)))
    incoming0_mid = jnp.where(jnp.isfinite(incoming0_mid), incoming0_mid, 0.0)
    fresh0_mid = down0_mid * incoming0_mid
    partial = jnp.dot(sel[0], jnp.sum(fresh0_mid, axis=(1, 2)), precision=lax.Precision.HIGHEST)
    update0_mid = mix(sel[0], fresh0_mid) / scaled0_mid
    (update0, incoming0), range_total = from_middle([update0_mid, incoming0_mid], partial)
    (picked, update0), total = fetch([(incoming0, 2), (update0, 1)], range_total)
    out0 = split_dot(sorting[2], t0_down0 * picked, transposed=True)
    t1_up0 = t1_up0 * (update0 * (sep_states / total))
    out1 = split_dot(sorting[1], t1_up0, transposed=True)
    t1_down1 = split_dot(down1_to_up0, t1_up0, transposed=True)
    (message,), total = send([(t1_down1, 3)])
    fresh1 = message * (sep_states / total)
    (fresh1_mid,) = to_middle([fresh1])
    (update1,), _ = from_middle([mix(sel[1], fresh1_mid) / scaled1_mid])
    (picked,), _ = fetch([(update1, 0)])
    out2 = split_dot(sorting[0], t2_up1 * picked, transposed=True)
    return jnp.stack([out0, out1, out2])[:, None]


def solution(mesh):
    return jax.shard_map(
        shards,
        mesh=mesh,
        in_specs=(
            P(None, "clique", "shard", None),
            P(None, "clique", "shard"),
            P(None, "clique", "shard"),
            P(),
        ),
        out_specs=P(None, "clique", "shard", None),
        check_vma=False,
    )
```

```python
import jax
import jax.numpy as jnp
from jax import lax
from jax.sharding import PartitionSpec as P

SEPB = 4096
PAD = 8


def split_dot(one_hot, x, transposed=False):
    lanes = x.shape[-1]
    hi = lax.reduce_precision(x, exponent_bits=8, mantissa_bits=7)
    lo = x - hi
    parts = jnp.concatenate([hi, lo], axis=1).astype(jnp.bfloat16)
    contract = 0 if transposed else 1
    y = lax.dot_general(
        one_hot, parts, (((contract,), (0,)), ((), ())), preferred_element_type=jnp.float32
    )
    return y[:, :lanes] + y[:, lanes:]


def one_hot_of(index, count):
    return (index[:, None] == jnp.arange(count, dtype=jnp.int32)[None, :]).astype(jnp.bfloat16)


def gather_rows(x, index):
    one_hot = (index[:, None] == jnp.arange(x.shape[0], dtype=jnp.int32)[None, :]).astype(
        jnp.bfloat16
    )
    return split_dot(one_hot, x)


def segment_rows(x, segment, count):
    one_hot = (jnp.arange(count, dtype=jnp.int32)[:, None] == segment[None, :]).astype(
        jnp.bfloat16
    )
    return split_dot(one_hot, x)


def shards(tables, up_map, down_map, parents):
    shard_count = lax.axis_size("shard")
    clique_count = lax.axis_size("clique")
    block_count = tables.shape[2]
    lane_count = tables.shape[3]
    per_owner = SEPB // shard_count
    per_peer = block_count // shard_count
    sep_states = float(SEPB * lane_count)

    lists = jnp.stack([up_map[1, 0], up_map[0, 0], down_map[0, 0], down_map[1, 0]])
    owner = lists // per_owner
    slot = lists % per_owner
    owned = (owner[:, :, None] == jnp.arange(shard_count, dtype=jnp.int32)).astype(jnp.bfloat16)
    earlier = (
        jnp.arange(block_count, dtype=jnp.int32)[:, None]
        >= jnp.arange(block_count, dtype=jnp.int32)[None, :]
    ).astype(jnp.bfloat16)
    owned_all = owned.transpose(1, 0, 2).reshape(block_count, 4 * shard_count)
    counts = jnp.dot(earlier, owned_all, preferred_element_type=jnp.float32)
    counts = counts.reshape(block_count, 4, shard_count).transpose(1, 0, 2)
    rank = jnp.sum(counts * owned.astype(jnp.float32), axis=2).astype(jnp.int32) - 1
    position = owner * per_peer + rank
    sorting = [
        (jnp.arange(block_count, dtype=jnp.int32)[:, None] == position[which][None, :]).astype(
            jnp.bfloat16
        )
        for which in range(4)
    ]
    halves = jnp.stack([slot // 32, slot % 32], axis=2).astype(jnp.bfloat16)
    sent_halves = jnp.einsum(
        "lib,lbh->lih", jnp.stack(sorting), halves, preferred_element_type=jnp.float32
    )
    sent_slots = (sent_halves[:, :, 0] * 32 + sent_halves[:, :, 1]).astype(jnp.int32)
    down1_to_up0 = lax.dot_general(
        sorting[1], sorting[3], (((1,), (1,)), ((), ())), preferred_element_type=jnp.float32
    ).astype(jnp.bfloat16)
    slot_rows = (4 * per_peer) // lane_count
    slot_chunk = (
        sent_slots.reshape(4, shard_count, per_peer)
        .transpose(1, 0, 2)
        .reshape(shard_count, slot_rows, lane_count)
        .astype(jnp.float32)
    )
    arrived = [None] * 4
    piece_rows = per_owner // clique_count

    def send(items, with_slots=False):
        partial_sum = jnp.sum(items[0][0])
        chunks = [rows.reshape(shard_count, per_peer, lane_count) for rows, _ in items]
        chunks.append(jnp.broadcast_to(partial_sum, (shard_count, PAD, lane_count)))
        if with_slots:
            chunks.append(slot_chunk)
        arrived_rows = lax.all_to_all(jnp.concatenate(chunks, axis=1), "shard", 0, 0, tiled=True)
        head = len(items) * per_peer
        total = jnp.sum(arrived_rows[:, head, 0])
        if with_slots:
            got = arrived_rows[:, head + PAD :].reshape(shard_count, 4, per_peer)
            got = got.transpose(1, 0, 2).reshape(4, block_count).astype(jnp.int32)
            for which in range(4):
                arrived[which] = got[which]
        messages = []
        for number, (_, which) in enumerate(items):
            rows = arrived_rows[:, number * per_peer : (number + 1) * per_peer]
            messages.append(
                segment_rows(rows.reshape(block_count, lane_count), arrived[which], per_owner)
            )
        return messages, total

    def fetch(items, partial=None):
        chunks = []
        for owned_rows, which in items:
            owned_rows = jnp.where(jnp.isfinite(owned_rows), owned_rows, 0.0)
            picked = gather_rows(owned_rows, arrived[which])
            chunks.append(picked.reshape(shard_count, per_peer, lane_count))
        if partial is not None:
            chunks.append(jnp.broadcast_to(partial, (shard_count, PAD, lane_count)))
        back = lax.all_to_all(jnp.concatenate(chunks, axis=1), "shard", 0, 0, tiled=True)
        rows = [
            back[:, number * per_peer : (number + 1) * per_peer].reshape(block_count, lane_count)
            for number in range(len(items))
        ]
        if partial is None:
            return rows, None
        return rows, jnp.sum(back[:, len(items) * per_peer, 0])

    def to_middle(arrays):
        pieces = [a.reshape(clique_count, piece_rows, lane_count) for a in arrays]
        got = lax.all_to_all(jnp.concatenate(pieces, axis=1), "clique", 0, 0, tiled=True)
        return [got[:, n * piece_rows : (n + 1) * piece_rows] for n in range(len(arrays))]

    def from_middle(arrays, partial=None):
        chunks = list(arrays)
        if partial is not None:
            chunks.append(jnp.broadcast_to(partial[:, None, None], (clique_count, PAD, lane_count)))
        got = lax.all_to_all(jnp.concatenate(chunks, axis=1), "clique", 0, 0, tiled=True)
        outs = [
            got[:, n * piece_rows : (n + 1) * piece_rows].reshape(per_owner, lane_count)
            for n in range(len(arrays))
        ]
        if partial is None:
            return outs, None
        return outs, jnp.sum(got[:, len(arrays) * piece_rows, 0])

    def mix(mixing, pieces):
        return jnp.einsum("oi,ixl->oxl", mixing, pieces, precision=lax.Precision.HIGHEST)

    clique_ids = jnp.arange(clique_count, dtype=jnp.int32)
    sel = [
        (parents[edge][:, None] == clique_ids[None, :]).astype(jnp.float32) for edge in (0, 1)
    ]
    t0, t1, t2 = tables[0, 0], tables[1, 0], tables[2, 0]

    t2_up1 = split_dot(sorting[0], t2)
    t0_down0 = split_dot(sorting[2], t0)
    (message, down0_message), total = send([(t2_up1, 0), (t0_down0, 2)], with_slots=True)
    scaled1 = message * (sep_states / total)
    scaled1_mid, down0_mid = to_middle([scaled1, down0_message])
    (incoming1,), _ = from_middle([jnp.exp(mix(sel[1].T, jnp.log(scaled1_mid)))])
    (picked,), _ = fetch([(incoming1, 3)])
    t1_down1 = split_dot(sorting[3], t1) * picked
    t1_up0 = split_dot(down1_to_up0, t1_down1)
    (message,), total = send([(t1_up0, 1)])
    scaled0 = message * (sep_states / total)
    (scaled0_mid,) = to_middle([scaled0])
    incoming0_mid = jnp.exp(mix(sel[0].T, jnp.log(scaled0_mid)))
    incoming0_mid = jnp.where(jnp.isfinite(incoming0_mid), incoming0_mid, 0.0)
    fresh0_mid = down0_mid * incoming0_mid
    partial = jnp.dot(sel[0], jnp.sum(fresh0_mid, axis=(1, 2)), precision=lax.Precision.HIGHEST)
    update0_mid = mix(sel[0], fresh0_mid) / scaled0_mid
    (update0, incoming0), range_total = from_middle([update0_mid, incoming0_mid], partial)
    (picked, update0), total = fetch([(incoming0, 2), (update0, 1)], range_total)
    out0 = split_dot(sorting[2], t0_down0 * picked, transposed=True)
    t1_up0 = t1_up0 * (update0 * (sep_states / total))
    out1 = split_dot(sorting[1], t1_up0, transposed=True)
    t1_down1 = split_dot(down1_to_up0, t1_up0, transposed=True)
    (message,), total = send([(t1_down1, 3)])
    fresh1 = message * (sep_states / total)
    (fresh1_mid,) = to_middle([fresh1])
    (update1,), _ = from_middle([mix(sel[1], fresh1_mid) / scaled1_mid])
    (picked,), _ = fetch([(update1, 0)])
    out2 = split_dot(sorting[0], t2_up1 * picked, transposed=True)
    return jnp.stack([out0, out1, out2])[:, None]


def solution(mesh):
    return jax.shard_map(
        shards,
        mesh=mesh,
        in_specs=(
            P(None, "clique", "shard", None),
            P(None, "clique", "shard"),
            P(None, "clique", "shard"),
            P(),
        ),
        out_specs=P(None, "clique", "shard", None),
        check_vma=False,
    )
```

```python
import jax
import jax.numpy as jnp
from jax import lax
from jax.sharding import PartitionSpec as P

SEPB = 4096
PAD = 8


def split_dot(one_hot, x, transposed=False):
    lanes = x.shape[-1]
    hi = lax.reduce_precision(x, exponent_bits=8, mantissa_bits=7)
    lo = x - hi
    parts = jnp.concatenate([hi, lo], axis=1).astype(jnp.bfloat16)
    contract = 0 if transposed else 1
    y = lax.dot_general(
        one_hot, parts, (((contract,), (0,)), ((), ())), preferred_element_type=jnp.float32
    )
    return y[:, :lanes] + y[:, lanes:]


def one_hot_of(index, count):
    return (index[:, None] == jnp.arange(count, dtype=jnp.int32)[None, :]).astype(jnp.bfloat16)


def gather_rows(x, index):
    one_hot = (index[:, None] == jnp.arange(x.shape[0], dtype=jnp.int32)[None, :]).astype(
        jnp.bfloat16
    )
    return split_dot(one_hot, x)


def segment_rows(x, segment, count):
    one_hot = (jnp.arange(count, dtype=jnp.int32)[:, None] == segment[None, :]).astype(
        jnp.bfloat16
    )
    return split_dot(one_hot, x)


def shards(tables, up_map, down_map, parents):
    shard_count = lax.axis_size("shard")
    clique_count = lax.axis_size("clique")
    block_count = tables.shape[2]
    lane_count = tables.shape[3]
    per_owner = SEPB // shard_count
    per_peer = block_count // shard_count
    sep_states = float(SEPB * lane_count)

    lists = jnp.stack([up_map[1, 0], up_map[0, 0], down_map[0, 0], down_map[1, 0]])
    owner = lists // per_owner
    slot = lists % per_owner
    owned = (owner[:, :, None] == jnp.arange(shard_count, dtype=jnp.int32)).astype(jnp.bfloat16)
    earlier = (
        jnp.arange(block_count, dtype=jnp.int32)[:, None]
        >= jnp.arange(block_count, dtype=jnp.int32)[None, :]
    ).astype(jnp.bfloat16)
    owned_all = owned.transpose(1, 0, 2).reshape(block_count, 4 * shard_count)
    counts = jnp.dot(earlier, owned_all, preferred_element_type=jnp.float32)
    counts = counts.reshape(block_count, 4, shard_count).transpose(1, 0, 2)
    rank = jnp.sum(counts * owned.astype(jnp.float32), axis=2).astype(jnp.int32) - 1
    position = owner * per_peer + rank
    sorting = [
        (jnp.arange(block_count, dtype=jnp.int32)[:, None] == position[which][None, :]).astype(
            jnp.bfloat16
        )
        for which in range(4)
    ]
    halves = jnp.stack([slot // 32, slot % 32], axis=2).astype(jnp.bfloat16)
    sent_halves = jnp.einsum(
        "lib,lbh->lih", jnp.stack(sorting), halves, preferred_element_type=jnp.float32
    )
    sent_slots = (sent_halves[:, :, 0] * 32 + sent_halves[:, :, 1]).astype(jnp.int32)
    down1_to_up0 = lax.dot_general(
        sorting[1], sorting[3], (((1,), (1,)), ((), ())), preferred_element_type=jnp.float32
    ).astype(jnp.bfloat16)
    slot_rows = (4 * per_peer) // lane_count
    slot_chunk = (
        sent_slots.reshape(4, shard_count, per_peer)
        .transpose(1, 0, 2)
        .reshape(shard_count, slot_rows, lane_count)
        .astype(jnp.float32)
    )
    arrived = [None] * 4
    piece_rows = per_owner // clique_count

    def send(items, with_slots=False):
        partial_sum = jnp.sum(items[0][0])
        chunks = [rows.reshape(shard_count, per_peer, lane_count) for rows, _ in items]
        chunks.append(jnp.broadcast_to(partial_sum, (shard_count, PAD, lane_count)))
        if with_slots:
            chunks.append(slot_chunk)
        arrived_rows = lax.all_to_all(jnp.concatenate(chunks, axis=1), "shard", 0, 0, tiled=True)
        head = len(items) * per_peer
        total = jnp.sum(arrived_rows[:, head, 0])
        if with_slots:
            got = arrived_rows[:, head + PAD :].reshape(shard_count, 4, per_peer)
            got = got.transpose(1, 0, 2).reshape(4, block_count).astype(jnp.int32)
            for which in range(4):
                arrived[which] = got[which]
        messages = []
        for number, (_, which) in enumerate(items):
            rows = arrived_rows[:, number * per_peer : (number + 1) * per_peer]
            messages.append(
                segment_rows(rows.reshape(block_count, lane_count), arrived[which], per_owner)
            )
        return messages, total

    def fetch(items, partial=None):
        chunks = []
        for owned_rows, which in items:
            owned_rows = jnp.where(jnp.isfinite(owned_rows), owned_rows, 0.0)
            picked = gather_rows(owned_rows, arrived[which])
            chunks.append(picked.reshape(shard_count, per_peer, lane_count))
        if partial is not None:
            chunks.append(jnp.broadcast_to(partial, (shard_count, PAD, lane_count)))
        back = lax.all_to_all(jnp.concatenate(chunks, axis=1), "shard", 0, 0, tiled=True)
        rows = [
            back[:, number * per_peer : (number + 1) * per_peer].reshape(block_count, lane_count)
            for number in range(len(items))
        ]
        if partial is None:
            return rows, None
        return rows, jnp.sum(back[:, len(items) * per_peer, 0])

    def to_middle(arrays):
        pieces = [a.reshape(clique_count, piece_rows, lane_count) for a in arrays]
        got = lax.all_to_all(jnp.concatenate(pieces, axis=1), "clique", 0, 0, tiled=True)
        return [got[:, n * piece_rows : (n + 1) * piece_rows] for n in range(len(arrays))]

    def from_middle(arrays, partial=None):
        chunks = list(arrays)
        if partial is not None:
            chunks.append(jnp.broadcast_to(partial[:, None, None], (clique_count, PAD, lane_count)))
        got = lax.all_to_all(jnp.concatenate(chunks, axis=1), "clique", 0, 0, tiled=True)
        outs = [
            got[:, n * piece_rows : (n + 1) * piece_rows].reshape(per_owner, lane_count)
            for n in range(len(arrays))
        ]
        if partial is None:
            return outs, None
        return outs, jnp.sum(got[:, len(arrays) * piece_rows, 0])

    def mix(mixing, pieces):
        return jnp.einsum("oi,ixl->oxl", mixing, pieces, precision=lax.Precision.HIGHEST)

    clique_ids = jnp.arange(clique_count, dtype=jnp.int32)
    sel = [
        (parents[edge][:, None] == clique_ids[None, :]).astype(jnp.float32) for edge in (0, 1)
    ]
    t0, t1, t2 = tables[0, 0], tables[1, 0], tables[2, 0]

    t2_up1 = split_dot(sorting[0], t2)
    t0_down0 = split_dot(sorting[2], t0)
    (message, down0_message), total = send([(t2_up1, 0), (t0_down0, 2)], with_slots=True)
    scaled1 = message * (sep_states / total)
    scaled1_mid, down0_mid = to_middle([scaled1, down0_message])
    (incoming1,), _ = from_middle([jnp.exp(mix(sel[1].T, jnp.log(scaled1_mid)))])
    (picked,), _ = fetch([(incoming1, 3)])
    t1_down1 = split_dot(sorting[3], t1) * picked
    t1_up0 = split_dot(down1_to_up0, t1_down1)
    (message,), total = send([(t1_up0, 1)])
    scaled0 = message * (sep_states / total)
    (scaled0_mid,) = to_middle([scaled0])
    incoming0_mid = jnp.exp(mix(sel[0].T, jnp.log(scaled0_mid)))
    incoming0_mid = jnp.where(jnp.isfinite(incoming0_mid), incoming0_mid, 0.0)
    fresh0_mid = down0_mid * incoming0_mid
    partial = jnp.dot(sel[0], jnp.sum(fresh0_mid, axis=(1, 2)), precision=lax.Precision.HIGHEST)
    update0_mid = mix(sel[0], fresh0_mid) / scaled0_mid
    (update0, incoming0), range_total = from_middle([update0_mid, incoming0_mid], partial)
    (update0,), total = fetch([(update0, 1)], range_total)
    incoming0 = lax.all_gather(incoming0, "shard", axis=0, tiled=True)
    out0 = t0 * gather_rows(incoming0, lists[2])
    t1_up0 = t1_up0 * (update0 * (sep_states / total))
    out1 = split_dot(sorting[1], t1_up0, transposed=True)
    t1_down1 = split_dot(down1_to_up0, t1_up0, transposed=True)
    (message,), total = send([(t1_down1, 3)])
    fresh1 = message * (sep_states / total)
    (fresh1_mid,) = to_middle([fresh1])
    (update1,), _ = from_middle([mix(sel[1], fresh1_mid) / scaled1_mid])
    (picked,), _ = fetch([(update1, 0)])
    out2 = split_dot(sorting[0], t2_up1 * picked, transposed=True)
    return jnp.stack([out0, out1, out2])[:, None]


def solution(mesh):
    return jax.shard_map(
        shards,
        mesh=mesh,
        in_specs=(
            P(None, "clique", "shard", None),
            P(None, "clique", "shard"),
            P(None, "clique", "shard"),
            P(),
        ),
        out_specs=P(None, "clique", "shard", None),
        check_vma=False,
    )
```

```python
import jax
import jax.numpy as jnp
from jax import lax
from jax.sharding import PartitionSpec as P

SEPB = 4096
PAD = 8


def split_dot(one_hot, x, transposed=False):
    lanes = x.shape[-1]
    hi = lax.reduce_precision(x, exponent_bits=8, mantissa_bits=7)
    lo = x - hi
    parts = jnp.concatenate([hi, lo], axis=1).astype(jnp.bfloat16)
    contract = 0 if transposed else 1
    y = lax.dot_general(
        one_hot, parts, (((contract,), (0,)), ((), ())), preferred_element_type=jnp.float32
    )
    return y[:, :lanes] + y[:, lanes:]


def one_hot_of(index, count):
    return (index[:, None] == jnp.arange(count, dtype=jnp.int32)[None, :]).astype(jnp.bfloat16)


def gather_rows(x, index):
    one_hot = (index[:, None] == jnp.arange(x.shape[0], dtype=jnp.int32)[None, :]).astype(
        jnp.bfloat16
    )
    return split_dot(one_hot, x)


def segment_rows(x, segment, count):
    one_hot = (jnp.arange(count, dtype=jnp.int32)[:, None] == segment[None, :]).astype(
        jnp.bfloat16
    )
    return split_dot(one_hot, x)


def shards(tables, up_map, down_map, parents):
    shard_count = lax.axis_size("shard")
    clique_count = lax.axis_size("clique")
    block_count = tables.shape[2]
    lane_count = tables.shape[3]
    per_owner = SEPB // shard_count
    per_peer = block_count // shard_count
    sep_states = float(SEPB * lane_count)

    lists = jnp.stack([up_map[1, 0], up_map[0, 0], down_map[0, 0], down_map[1, 0]])
    owner = lists // per_owner
    slot = lists % per_owner
    owned = (owner[:, :, None] == jnp.arange(shard_count, dtype=jnp.int32)).astype(jnp.bfloat16)
    earlier = (
        jnp.arange(block_count, dtype=jnp.int32)[:, None]
        >= jnp.arange(block_count, dtype=jnp.int32)[None, :]
    ).astype(jnp.bfloat16)
    owned_all = owned.transpose(1, 0, 2).reshape(block_count, 4 * shard_count)
    counts = jnp.dot(earlier, owned_all, preferred_element_type=jnp.float32)
    counts = counts.reshape(block_count, 4, shard_count).transpose(1, 0, 2)
    rank = jnp.sum(counts * owned.astype(jnp.float32), axis=2).astype(jnp.int32) - 1
    position = owner * per_peer + rank
    sorting = [
        (jnp.arange(block_count, dtype=jnp.int32)[:, None] == position[which][None, :]).astype(
            jnp.bfloat16
        )
        for which in range(4)
    ]
    halves = jnp.stack([slot // 32, slot % 32], axis=2).astype(jnp.bfloat16)
    placed = (
        position[:, :, None] == jnp.arange(block_count, dtype=jnp.int32)[None, None, :]
    ).astype(jnp.bfloat16)
    sent_halves = jnp.einsum("lbi,lbh->lih", placed, halves, preferred_element_type=jnp.float32)
    sent_slots = (sent_halves[:, :, 0] * 32 + sent_halves[:, :, 1]).astype(jnp.int32)
    down1_to_up0 = lax.dot_general(
        sorting[1], sorting[3], (((1,), (1,)), ((), ())), preferred_element_type=jnp.float32
    ).astype(jnp.bfloat16)
    slot_rows = (4 * per_peer) // lane_count
    slot_chunk = (
        sent_slots.reshape(4, shard_count, per_peer)
        .transpose(1, 0, 2)
        .reshape(shard_count, slot_rows, lane_count)
        .astype(jnp.float32)
    )
    arrived = [None] * 4
    piece_rows = per_owner // clique_count

    def send(items, with_slots=False):
        partial_sum = jnp.sum(items[0][0])
        chunks = [rows.reshape(shard_count, per_peer, lane_count) for rows, _ in items]
        chunks.append(jnp.broadcast_to(partial_sum, (shard_count, PAD, lane_count)))
        if with_slots:
            chunks.append(slot_chunk)
        arrived_rows = lax.all_to_all(jnp.concatenate(chunks, axis=1), "shard", 0, 0, tiled=True)
        head = len(items) * per_peer
        total = jnp.sum(arrived_rows[:, head, 0])
        if with_slots:
            got = arrived_rows[:, head + PAD :].reshape(shard_count, 4, per_peer)
            got = got.transpose(1, 0, 2).reshape(4, block_count).astype(jnp.int32)
            for which in range(4):
                arrived[which] = got[which]
        messages = []
        for number, (_, which) in enumerate(items):
            rows = arrived_rows[:, number * per_peer : (number + 1) * per_peer]
            messages.append(
                segment_rows(rows.reshape(block_count, lane_count), arrived[which], per_owner)
            )
        return messages, total

    def fetch(items, partial=None):
        chunks = []
        for owned_rows, which in items:
            owned_rows = jnp.where(jnp.isfinite(owned_rows), owned_rows, 0.0)
            picked = gather_rows(owned_rows, arrived[which])
            chunks.append(picked.reshape(shard_count, per_peer, lane_count))
        if partial is not None:
            chunks.append(jnp.broadcast_to(partial, (shard_count, PAD, lane_count)))
        back = lax.all_to_all(jnp.concatenate(chunks, axis=1), "shard", 0, 0, tiled=True)
        rows = [
            back[:, number * per_peer : (number + 1) * per_peer].reshape(block_count, lane_count)
            for number in range(len(items))
        ]
        if partial is None:
            return rows, None
        return rows, jnp.sum(back[:, len(items) * per_peer, 0])

    def to_middle(arrays):
        pieces = [a.reshape(clique_count, piece_rows, lane_count) for a in arrays]
        got = lax.all_to_all(jnp.concatenate(pieces, axis=1), "clique", 0, 0, tiled=True)
        return [got[:, n * piece_rows : (n + 1) * piece_rows] for n in range(len(arrays))]

    def from_middle(arrays, partial=None):
        chunks = list(arrays)
        if partial is not None:
            chunks.append(jnp.broadcast_to(partial[:, None, None], (clique_count, PAD, lane_count)))
        got = lax.all_to_all(jnp.concatenate(chunks, axis=1), "clique", 0, 0, tiled=True)
        outs = [
            got[:, n * piece_rows : (n + 1) * piece_rows].reshape(per_owner, lane_count)
            for n in range(len(arrays))
        ]
        if partial is None:
            return outs, None
        return outs, jnp.sum(got[:, len(arrays) * piece_rows, 0])

    def mix(mixing, pieces):
        return jnp.einsum("oi,ixl->oxl", mixing, pieces, precision=lax.Precision.HIGHEST)

    clique_ids = jnp.arange(clique_count, dtype=jnp.int32)
    sel = [
        (parents[edge][:, None] == clique_ids[None, :]).astype(jnp.float32) for edge in (0, 1)
    ]
    t0, t1, t2 = tables[0, 0], tables[1, 0], tables[2, 0]

    t2_up1 = split_dot(sorting[0], t2)
    t0_down0 = split_dot(sorting[2], t0)
    (message, down0_message), total = send([(t2_up1, 0), (t0_down0, 2)], with_slots=True)
    scaled1 = message * (sep_states / total)
    scaled1_mid, down0_mid = to_middle([scaled1, down0_message])
    (incoming1,), _ = from_middle([jnp.exp(mix(sel[1].T, jnp.log(scaled1_mid)))])
    (picked,), _ = fetch([(incoming1, 3)])
    t1_down1 = split_dot(sorting[3], t1) * picked
    t1_up0 = split_dot(down1_to_up0, t1_down1)
    (message,), total = send([(t1_up0, 1)])
    scaled0 = message * (sep_states / total)
    (scaled0_mid,) = to_middle([scaled0])
    incoming0_mid = jnp.exp(mix(sel[0].T, jnp.log(scaled0_mid)))
    incoming0_mid = jnp.where(jnp.isfinite(incoming0_mid), incoming0_mid, 0.0)
    fresh0_mid = down0_mid * incoming0_mid
    partial = jnp.dot(sel[0], jnp.sum(fresh0_mid, axis=(1, 2)), precision=lax.Precision.HIGHEST)
    update0_mid = mix(sel[0], fresh0_mid) / scaled0_mid
    (update0, incoming0), range_total = from_middle([update0_mid, incoming0_mid], partial)
    (picked, update0), total = fetch([(incoming0, 2), (update0, 1)], range_total)
    out0 = split_dot(sorting[2], t0_down0 * picked, transposed=True)
    t1_up0 = t1_up0 * (update0 * (sep_states / total))
    out1 = split_dot(sorting[1], t1_up0, transposed=True)
    t1_down1 = split_dot(down1_to_up0, t1_up0, transposed=True)
    (message,), total = send([(t1_down1, 3)])
    fresh1 = message * (sep_states / total)
    (fresh1_mid,) = to_middle([fresh1])
    (update1,), _ = from_middle([mix(sel[1], fresh1_mid) / scaled1_mid])
    (picked,), _ = fetch([(update1, 0)])
    out2 = split_dot(sorting[0], t2_up1 * picked, transposed=True)
    return jnp.stack([out0, out1, out2])[:, None]


def solution(mesh):
    return jax.shard_map(
        shards,
        mesh=mesh,
        in_specs=(
            P(None, "clique", "shard", None),
            P(None, "clique", "shard"),
            P(None, "clique", "shard"),
            P(),
        ),
        out_specs=P(None, "clique", "shard", None),
        check_vma=False,
    )
```

```python
import jax
import jax.numpy as jnp
from jax import lax
from jax.sharding import PartitionSpec as P

SEPB = 4096
PAD = 8


def split_dot(one_hot, x, transposed=False):
    lanes = x.shape[-1]
    hi = lax.reduce_precision(x, exponent_bits=8, mantissa_bits=7)
    lo = x - hi
    parts = jnp.concatenate([hi, lo], axis=1).astype(jnp.bfloat16)
    contract = 0 if transposed else 1
    y = lax.dot_general(
        one_hot, parts, (((contract,), (0,)), ((), ())), preferred_element_type=jnp.float32
    )
    return y[:, :lanes] + y[:, lanes:]


def one_hot_of(index, count):
    return (index[:, None] == jnp.arange(count, dtype=jnp.int32)[None, :]).astype(jnp.bfloat16)


def gather_rows(x, index):
    one_hot = (index[:, None] == jnp.arange(x.shape[0], dtype=jnp.int32)[None, :]).astype(
        jnp.bfloat16
    )
    return split_dot(one_hot, x)


def segment_rows(x, segment, count):
    one_hot = (jnp.arange(count, dtype=jnp.int32)[:, None] == segment[None, :]).astype(
        jnp.bfloat16
    )
    return split_dot(one_hot, x)


def shards(tables, up_map, down_map, parents):
    shard_count = lax.axis_size("shard")
    clique_count = lax.axis_size("clique")
    block_count = tables.shape[2]
    lane_count = tables.shape[3]
    per_owner = SEPB // shard_count
    per_peer = block_count // shard_count
    sep_states = float(SEPB * lane_count)

    lists = jnp.stack([up_map[1, 0], up_map[0, 0], down_map[0, 0], down_map[1, 0]])
    owner = lists // per_owner
    slot = lists % per_owner
    owned = (owner[:, :, None] == jnp.arange(shard_count, dtype=jnp.int32)).astype(jnp.bfloat16)
    earlier = (
        jnp.arange(block_count, dtype=jnp.int32)[:, None]
        >= jnp.arange(block_count, dtype=jnp.int32)[None, :]
    ).astype(jnp.bfloat16)
    owned_all = owned.transpose(1, 0, 2).reshape(block_count, 4 * shard_count)
    counts = jnp.dot(earlier, owned_all, preferred_element_type=jnp.float32)
    counts = counts.reshape(block_count, 4, shard_count).transpose(1, 0, 2)
    rank = jnp.sum(counts * owned.astype(jnp.float32), axis=2).astype(jnp.int32) - 1
    position = owner * per_peer + rank
    sorting = [
        (jnp.arange(block_count, dtype=jnp.int32)[:, None] == position[which][None, :]).astype(
            jnp.bfloat16
        )
        for which in range(4)
    ]
    halves = jnp.stack([slot // 32, slot % 32], axis=2).astype(jnp.bfloat16)
    high = (
        (position // 32)[:, None, :] == jnp.arange(block_count // 32, dtype=jnp.int32)[None, :, None]
    ).astype(jnp.bfloat16)
    low = (
        (position % 32)[:, :, None] == jnp.arange(32, dtype=jnp.int32)[None, None, :]
    ).astype(jnp.bfloat16)
    spread = (low[:, :, :, None] * halves[:, :, None, :]).reshape(4, block_count, 64)
    sent_halves = jnp.einsum("lkb,lbn->lkn", high, spread, preferred_element_type=jnp.float32)
    sent_halves = sent_halves.reshape(4, block_count, 2)
    sent_slots = (sent_halves[:, :, 0] * 32 + sent_halves[:, :, 1]).astype(jnp.int32)
    down1_to_up0 = lax.dot_general(
        sorting[1], sorting[3], (((1,), (1,)), ((), ())), preferred_element_type=jnp.float32
    ).astype(jnp.bfloat16)
    slot_rows = (4 * per_peer) // lane_count
    slot_chunk = (
        sent_slots.reshape(4, shard_count, per_peer)
        .transpose(1, 0, 2)
        .reshape(shard_count, slot_rows, lane_count)
        .astype(jnp.float32)
    )
    arrived = [None] * 4
    piece_rows = per_owner // clique_count

    def send(items, with_slots=False):
        partial_sum = jnp.sum(items[0][0])
        chunks = [rows.reshape(shard_count, per_peer, lane_count) for rows, _ in items]
        chunks.append(jnp.broadcast_to(partial_sum, (shard_count, PAD, lane_count)))
        if with_slots:
            chunks.append(slot_chunk)
        arrived_rows = lax.all_to_all(jnp.concatenate(chunks, axis=1), "shard", 0, 0, tiled=True)
        head = len(items) * per_peer
        total = jnp.sum(arrived_rows[:, head, 0])
        if with_slots:
            got = arrived_rows[:, head + PAD :].reshape(shard_count, 4, per_peer)
            got = got.transpose(1, 0, 2).reshape(4, block_count).astype(jnp.int32)
            for which in range(4):
                arrived[which] = got[which]
        messages = []
        for number, (_, which) in enumerate(items):
            rows = arrived_rows[:, number * per_peer : (number + 1) * per_peer]
            messages.append(
                segment_rows(rows.reshape(block_count, lane_count), arrived[which], per_owner)
            )
        return messages, total

    def fetch(items, partial=None):
        chunks = []
        for owned_rows, which in items:
            owned_rows = jnp.where(jnp.isfinite(owned_rows), owned_rows, 0.0)
            picked = gather_rows(owned_rows, arrived[which])
            chunks.append(picked.reshape(shard_count, per_peer, lane_count))
        if partial is not None:
            chunks.append(jnp.broadcast_to(partial, (shard_count, PAD, lane_count)))
        back = lax.all_to_all(jnp.concatenate(chunks, axis=1), "shard", 0, 0, tiled=True)
        rows = [
            back[:, number * per_peer : (number + 1) * per_peer].reshape(block_count, lane_count)
            for number in range(len(items))
        ]
        if partial is None:
            return rows, None
        return rows, jnp.sum(back[:, len(items) * per_peer, 0])

    def to_middle(arrays):
        pieces = [a.reshape(clique_count, piece_rows, lane_count) for a in arrays]
        got = lax.all_to_all(jnp.concatenate(pieces, axis=1), "clique", 0, 0, tiled=True)
        return [got[:, n * piece_rows : (n + 1) * piece_rows] for n in range(len(arrays))]

    def from_middle(arrays, partial=None):
        chunks = list(arrays)
        if partial is not None:
            chunks.append(jnp.broadcast_to(partial[:, None, None], (clique_count, PAD, lane_count)))
        got = lax.all_to_all(jnp.concatenate(chunks, axis=1), "clique", 0, 0, tiled=True)
        outs = [
            got[:, n * piece_rows : (n + 1) * piece_rows].reshape(per_owner, lane_count)
            for n in range(len(arrays))
        ]
        if partial is None:
            return outs, None
        return outs, jnp.sum(got[:, len(arrays) * piece_rows, 0])

    def mix(mixing, pieces):
        return jnp.einsum("oi,ixl->oxl", mixing, pieces, precision=lax.Precision.HIGHEST)

    clique_ids = jnp.arange(clique_count, dtype=jnp.int32)
    sel = [
        (parents[edge][:, None] == clique_ids[None, :]).astype(jnp.float32) for edge in (0, 1)
    ]
    t0, t1, t2 = tables[0, 0], tables[1, 0], tables[2, 0]

    t2_up1 = split_dot(sorting[0], t2)
    t0_down0 = split_dot(sorting[2], t0)
    (message, down0_message), total = send([(t2_up1, 0), (t0_down0, 2)], with_slots=True)
    scaled1 = message * (sep_states / total)
    scaled1_mid, down0_mid = to_middle([scaled1, down0_message])
    (incoming1,), _ = from_middle([jnp.exp(mix(sel[1].T, jnp.log(scaled1_mid)))])
    (picked,), _ = fetch([(incoming1, 3)])
    t1_down1 = split_dot(sorting[3], t1) * picked
    t1_up0 = split_dot(down1_to_up0, t1_down1)
    (message,), total = send([(t1_up0, 1)])
    scaled0 = message * (sep_states / total)
    (scaled0_mid,) = to_middle([scaled0])
    incoming0_mid = jnp.exp(mix(sel[0].T, jnp.log(scaled0_mid)))
    incoming0_mid = jnp.where(jnp.isfinite(incoming0_mid), incoming0_mid, 0.0)
    fresh0_mid = down0_mid * incoming0_mid
    partial = jnp.dot(sel[0], jnp.sum(fresh0_mid, axis=(1, 2)), precision=lax.Precision.HIGHEST)
    update0_mid = mix(sel[0], fresh0_mid) / scaled0_mid
    (update0, incoming0), range_total = from_middle([update0_mid, incoming0_mid], partial)
    (picked, update0), total = fetch([(incoming0, 2), (update0, 1)], range_total)
    out0 = split_dot(sorting[2], t0_down0 * picked, transposed=True)
    t1_up0 = t1_up0 * (update0 * (sep_states / total))
    out1 = split_dot(sorting[1], t1_up0, transposed=True)
    t1_down1 = split_dot(down1_to_up0, t1_up0, transposed=True)
    (message,), total = send([(t1_down1, 3)])
    fresh1 = message * (sep_states / total)
    (fresh1_mid,) = to_middle([fresh1])
    (update1,), _ = from_middle([mix(sel[1], fresh1_mid) / scaled1_mid])
    (picked,), _ = fetch([(update1, 0)])
    out2 = split_dot(sorting[0], t2_up1 * picked, transposed=True)
    return jnp.stack([out0, out1, out2])[:, None]


def solution(mesh):
    return jax.shard_map(
        shards,
        mesh=mesh,
        in_specs=(
            P(None, "clique", "shard", None),
            P(None, "clique", "shard"),
            P(None, "clique", "shard"),
            P(),
        ),
        out_specs=P(None, "clique", "shard", None),
        check_vma=False,
    )
```

```python
import jax
import jax.numpy as jnp
from jax import lax
from jax.sharding import PartitionSpec as P

SEPB = 4096
PAD = 8


def split_dot(one_hot, x, transposed=False):
    lanes = x.shape[-1]
    hi = lax.reduce_precision(x, exponent_bits=8, mantissa_bits=7)
    lo = x - hi
    parts = jnp.concatenate([hi, lo], axis=1).astype(jnp.bfloat16)
    contract = 0 if transposed else 1
    y = lax.dot_general(
        one_hot, parts, (((contract,), (0,)), ((), ())), preferred_element_type=jnp.float32
    )
    return y[:, :lanes] + y[:, lanes:]


def one_hot_of(index, count):
    return (index[:, None] == jnp.arange(count, dtype=jnp.int32)[None, :]).astype(jnp.bfloat16)


def gather_rows(x, index):
    one_hot = (index[:, None] == jnp.arange(x.shape[0], dtype=jnp.int32)[None, :]).astype(
        jnp.bfloat16
    )
    return split_dot(one_hot, x)


def segment_rows(x, segment, count):
    one_hot = (jnp.arange(count, dtype=jnp.int32)[:, None] == segment[None, :]).astype(
        jnp.bfloat16
    )
    return split_dot(one_hot, x)


def shards(tables, up_map, down_map, parents):
    shard_count = lax.axis_size("shard")
    clique_count = lax.axis_size("clique")
    block_count = tables.shape[2]
    lane_count = tables.shape[3]
    per_owner = SEPB // shard_count
    per_peer = block_count // shard_count
    sep_states = float(SEPB * lane_count)

    lists = jnp.stack([up_map[1, 0], up_map[0, 0], down_map[0, 0], down_map[1, 0]])
    owner = lists // per_owner
    slot = lists % per_owner
    owned = (owner[:, :, None] == jnp.arange(shard_count, dtype=jnp.int32)).astype(jnp.bfloat16)
    earlier = (
        jnp.arange(block_count, dtype=jnp.int32)[:, None]
        >= jnp.arange(block_count, dtype=jnp.int32)[None, :]
    ).astype(jnp.bfloat16)
    owned_all = owned.transpose(1, 0, 2).reshape(block_count, 4 * shard_count)
    counts = jnp.dot(earlier, owned_all, preferred_element_type=jnp.float32)
    counts = counts.reshape(block_count, 4, shard_count).transpose(1, 0, 2)
    rank = jnp.sum(counts * owned.astype(jnp.float32), axis=2).astype(jnp.int32) - 1
    position = owner * per_peer + rank
    sorting = [
        (jnp.arange(block_count, dtype=jnp.int32)[:, None] == position[which][None, :]).astype(
            jnp.bfloat16
        )
        for which in range(4)
    ]
    halves = jnp.stack([slot // 32, slot % 32], axis=2).astype(jnp.bfloat16)
    placed = (
        position[:, :, None] == jnp.arange(block_count, dtype=jnp.int32)[None, None, :]
    ).astype(jnp.bfloat16)
    sent_halves = jnp.einsum("lbi,lbh->lih", placed, halves, preferred_element_type=jnp.float32)
    sent_slots = (sent_halves[:, :, 0] * 32 + sent_halves[:, :, 1]).astype(jnp.int32)
    down1_to_up0 = lax.dot_general(
        sorting[1], sorting[3], (((1,), (1,)), ((), ())), preferred_element_type=jnp.float32
    ).astype(jnp.bfloat16)
    slot_rows = (4 * per_peer) // lane_count
    slot_chunk = (
        sent_slots.reshape(4, shard_count, per_peer)
        .transpose(1, 0, 2)
        .reshape(shard_count, slot_rows, lane_count)
        .astype(jnp.float32)
    )
    arrived = [None] * 4
    piece_rows = per_owner // clique_count

    def send(items, with_slots=False):
        partial_sum = jnp.sum(items[0][0])
        chunks = [rows.reshape(shard_count, per_peer, lane_count) for rows, _ in items]
        chunks.append(jnp.broadcast_to(partial_sum, (shard_count, PAD, lane_count)))
        if with_slots:
            chunks.append(slot_chunk)
        arrived_rows = lax.all_to_all(jnp.concatenate(chunks, axis=1), "shard", 0, 0, tiled=True)
        head = len(items) * per_peer
        total = jnp.sum(arrived_rows[:, head, 0])
        if with_slots:
            got = arrived_rows[:, head + PAD :].reshape(shard_count, 4, per_peer)
            got = got.transpose(1, 0, 2).reshape(4, block_count).astype(jnp.int32)
            for which in range(4):
                arrived[which] = got[which]
        messages = []
        for number, (_, which) in enumerate(items):
            rows = arrived_rows[:, number * per_peer : (number + 1) * per_peer]
            messages.append(
                segment_rows(rows.reshape(block_count, lane_count), arrived[which], per_owner)
            )
        return messages, total

    def fetch(items, partial=None, extra=None):
        chunks = [] if extra is None else [extra.reshape(shard_count, per_peer, lane_count)]
        for owned_rows, which in items:
            owned_rows = jnp.where(jnp.isfinite(owned_rows), owned_rows, 0.0)
            picked = gather_rows(owned_rows, arrived[which])
            chunks.append(picked.reshape(shard_count, per_peer, lane_count))
        if partial is not None:
            chunks.append(jnp.broadcast_to(partial, (shard_count, PAD, lane_count)))
        back = lax.all_to_all(jnp.concatenate(chunks, axis=1), "shard", 0, 0, tiled=True)
        count = len(items) + (extra is not None)
        rows = [
            back[:, number * per_peer : (number + 1) * per_peer].reshape(block_count, lane_count)
            for number in range(count)
        ]
        if partial is None:
            return rows, None
        return rows, jnp.sum(back[:, count * per_peer, 0])

    def to_middle(arrays):
        pieces = [a.reshape(clique_count, piece_rows, lane_count) for a in arrays]
        got = lax.all_to_all(jnp.concatenate(pieces, axis=1), "clique", 0, 0, tiled=True)
        return [got[:, n * piece_rows : (n + 1) * piece_rows] for n in range(len(arrays))]

    def from_middle(arrays, partial=None):
        chunks = list(arrays)
        if partial is not None:
            chunks.append(jnp.broadcast_to(partial[:, None, None], (clique_count, PAD, lane_count)))
        got = lax.all_to_all(jnp.concatenate(chunks, axis=1), "clique", 0, 0, tiled=True)
        outs = [
            got[:, n * piece_rows : (n + 1) * piece_rows].reshape(per_owner, lane_count)
            for n in range(len(arrays))
        ]
        if partial is None:
            return outs, None
        return outs, jnp.sum(got[:, len(arrays) * piece_rows, 0])

    def mix(mixing, pieces):
        return jnp.einsum("oi,ixl->oxl", mixing, pieces, precision=lax.Precision.HIGHEST)

    clique_ids = jnp.arange(clique_count, dtype=jnp.int32)
    sel = [
        (parents[edge][:, None] == clique_ids[None, :]).astype(jnp.float32) for edge in (0, 1)
    ]
    t0, t1, t2 = tables[0, 0], tables[1, 0], tables[2, 0]

    t2_up1 = split_dot(sorting[0], t2)
    (message,), total = send([(t2_up1, 0)], with_slots=True)
    scaled1 = message * (sep_states / total)
    (scaled1_mid,) = to_middle([scaled1])
    (incoming1,), _ = from_middle([jnp.exp(mix(sel[1].T, jnp.log(scaled1_mid)))])
    t0_down0 = split_dot(sorting[2], t0)
    (level0_rows, picked), _ = fetch([(incoming1, 3)], extra=t0_down0)
    down0_message = segment_rows(level0_rows, arrived[2], per_owner)
    t1_down1 = split_dot(sorting[3], t1) * picked
    t1_up0 = split_dot(down1_to_up0, t1_down1)
    (message,), total = send([(t1_up0, 1)])
    scaled0 = message * (sep_states / total)
    scaled0_mid, down0_mid = to_middle([scaled0, down0_message])
    incoming0_mid = jnp.exp(mix(sel[0].T, jnp.log(scaled0_mid)))
    incoming0_mid = jnp.where(jnp.isfinite(incoming0_mid), incoming0_mid, 0.0)
    fresh0_mid = down0_mid * incoming0_mid
    partial = jnp.dot(sel[0], jnp.sum(fresh0_mid, axis=(1, 2)), precision=lax.Precision.HIGHEST)
    update0_mid = mix(sel[0], fresh0_mid) / scaled0_mid
    (update0, incoming0), range_total = from_middle([update0_mid, incoming0_mid], partial)
    (picked, update0), total = fetch([(incoming0, 2), (update0, 1)], range_total)
    out0 = split_dot(sorting[2], t0_down0 * picked, transposed=True)
    t1_up0 = t1_up0 * (update0 * (sep_states / total))
    out1 = split_dot(sorting[1], t1_up0, transposed=True)
    t1_down1 = split_dot(down1_to_up0, t1_up0, transposed=True)
    (message,), total = send([(t1_down1, 3)])
    fresh1 = message * (sep_states / total)
    (fresh1_mid,) = to_middle([fresh1])
    (update1,), _ = from_middle([mix(sel[1], fresh1_mid) / scaled1_mid])
    (picked,), _ = fetch([(update1, 0)])
    out2 = split_dot(sorting[0], t2_up1 * picked, transposed=True)
    return jnp.stack([out0, out1, out2])[:, None]


def solution(mesh):
    return jax.shard_map(
        shards,
        mesh=mesh,
        in_specs=(
            P(None, "clique", "shard", None),
            P(None, "clique", "shard"),
            P(None, "clique", "shard"),
            P(),
        ),
        out_specs=P(None, "clique", "shard", None),
        check_vma=False,
    )
```

```python
import jax
import jax.numpy as jnp
from jax import lax
from jax.sharding import PartitionSpec as P

SEPB = 4096
PAD = 8


def split_dot(one_hot, x, transposed=False):
    lanes = x.shape[-1]
    hi = lax.reduce_precision(x, exponent_bits=8, mantissa_bits=7)
    lo = x - hi
    parts = jnp.concatenate([hi, lo], axis=1).astype(jnp.bfloat16)
    contract = 0 if transposed else 1
    y = lax.dot_general(
        one_hot, parts, (((contract,), (0,)), ((), ())), preferred_element_type=jnp.float32
    )
    return y[:, :lanes] + y[:, lanes:]


def one_hot_of(index, count):
    return (index[:, None] == jnp.arange(count, dtype=jnp.int32)[None, :]).astype(jnp.bfloat16)


def gather_rows(x, index):
    one_hot = (index[:, None] == jnp.arange(x.shape[0], dtype=jnp.int32)[None, :]).astype(
        jnp.bfloat16
    )
    return split_dot(one_hot, x)


def segment_rows(x, segment, count):
    one_hot = (jnp.arange(count, dtype=jnp.int32)[:, None] == segment[None, :]).astype(
        jnp.bfloat16
    )
    return split_dot(one_hot, x)


def shards(tables, up_map, down_map, parents):
    shard_count = lax.axis_size("shard")
    clique_count = lax.axis_size("clique")
    block_count = tables.shape[2]
    lane_count = tables.shape[3]
    per_owner = SEPB // shard_count
    per_peer = block_count // shard_count
    sep_states = float(SEPB * lane_count)

    lists = jnp.stack([up_map[1, 0], up_map[0, 0], down_map[0, 0], down_map[1, 0]])
    owner = lists // per_owner
    slot = lists % per_owner
    owned = (owner[:, :, None] == jnp.arange(shard_count, dtype=jnp.int32)).astype(jnp.bfloat16)
    earlier = (
        jnp.arange(block_count, dtype=jnp.int32)[:, None]
        >= jnp.arange(block_count, dtype=jnp.int32)[None, :]
    ).astype(jnp.bfloat16)
    owned_all = owned.transpose(1, 0, 2).reshape(block_count, 4 * shard_count)
    counts = jnp.dot(earlier, owned_all, preferred_element_type=jnp.float32)
    counts = counts.reshape(block_count, 4, shard_count).transpose(1, 0, 2)
    rank = jnp.sum(counts * owned.astype(jnp.float32), axis=2).astype(jnp.int32) - 1
    position = owner * per_peer + rank
    sorting = [
        (jnp.arange(block_count, dtype=jnp.int32)[:, None] == position[which][None, :]).astype(
            jnp.bfloat16
        )
        for which in range(4)
    ]
    halves = jnp.stack([slot // 32, slot % 32], axis=2).astype(jnp.bfloat16)

    def slot_chunk_of(which):
        placed = (
            position[jnp.array(which), :, None] == jnp.arange(block_count, dtype=jnp.int32)[None, None, :]
        ).astype(jnp.bfloat16)
        got = jnp.einsum("lbi,lbh->lih", placed, halves[jnp.array(which)], preferred_element_type=jnp.float32)
        sent = got[:, :, 0] * 32 + got[:, :, 1]
        rows = (len(which) * per_peer) // lane_count
        return (
            sent.reshape(len(which), shard_count, per_peer)
            .transpose(1, 0, 2)
            .reshape(shard_count, rows, lane_count)
        )

    def take_slots(received, which):
        got = received.reshape(shard_count, len(which), per_peer).transpose(1, 0, 2)
        got = got.reshape(len(which), block_count).astype(jnp.int32)
        for number, list_number in enumerate(which):
            arrived[list_number] = got[number]

    down1_to_up0 = lax.dot_general(
        sorting[1], sorting[3], (((1,), (1,)), ((), ())), preferred_element_type=jnp.float32
    ).astype(jnp.bfloat16)
    arrived = [None] * 4
    piece_rows = per_owner // clique_count

    def send(items, with_slots=False):
        partial_sum = jnp.sum(items[0][0])
        chunks = [rows.reshape(shard_count, per_peer, lane_count) for rows, _ in items]
        chunks.append(jnp.broadcast_to(partial_sum, (shard_count, PAD, lane_count)))
        if with_slots:
            chunks.append(slot_chunk_of([0, 3]))
        arrived_rows = lax.all_to_all(jnp.concatenate(chunks, axis=1), "shard", 0, 0, tiled=True)
        head = len(items) * per_peer
        total = jnp.sum(arrived_rows[:, head, 0])
        if with_slots:
            take_slots(arrived_rows[:, head + PAD :], [0, 3])
        messages = []
        for number, (_, which) in enumerate(items):
            rows = arrived_rows[:, number * per_peer : (number + 1) * per_peer]
            messages.append(
                segment_rows(rows.reshape(block_count, lane_count), arrived[which], per_owner)
            )
        return messages, total

    def fetch(items, partial=None, extra=None):
        chunks = []
        if extra is not None:
            chunks = [extra.reshape(shard_count, per_peer, lane_count), slot_chunk_of([1, 2])]
        slot_count = 0 if extra is None else chunks[1].shape[1]
        for owned_rows, which in items:
            owned_rows = jnp.where(jnp.isfinite(owned_rows), owned_rows, 0.0)
            picked = gather_rows(owned_rows, arrived[which])
            chunks.append(picked.reshape(shard_count, per_peer, lane_count))
        if partial is not None:
            chunks.append(jnp.broadcast_to(partial, (shard_count, PAD, lane_count)))
        back = lax.all_to_all(jnp.concatenate(chunks, axis=1), "shard", 0, 0, tiled=True)
        if extra is not None:
            take_slots(back[:, per_peer : per_peer + slot_count], [1, 2])
            back = jnp.concatenate([back[:, :per_peer], back[:, per_peer + slot_count :]], axis=1)
        count = len(items) + (extra is not None)
        rows = [
            back[:, number * per_peer : (number + 1) * per_peer].reshape(block_count, lane_count)
            for number in range(count)
        ]
        if partial is None:
            return rows, None
        return rows, jnp.sum(back[:, count * per_peer, 0])

    def to_middle(arrays):
        pieces = [a.reshape(clique_count, piece_rows, lane_count) for a in arrays]
        got = lax.all_to_all(jnp.concatenate(pieces, axis=1), "clique", 0, 0, tiled=True)
        return [got[:, n * piece_rows : (n + 1) * piece_rows] for n in range(len(arrays))]

    def from_middle(arrays, partial=None):
        chunks = list(arrays)
        if partial is not None:
            chunks.append(jnp.broadcast_to(partial[:, None, None], (clique_count, PAD, lane_count)))
        got = lax.all_to_all(jnp.concatenate(chunks, axis=1), "clique", 0, 0, tiled=True)
        outs = [
            got[:, n * piece_rows : (n + 1) * piece_rows].reshape(per_owner, lane_count)
            for n in range(len(arrays))
        ]
        if partial is None:
            return outs, None
        return outs, jnp.sum(got[:, len(arrays) * piece_rows, 0])

    def mix(mixing, pieces):
        return jnp.einsum("oi,ixl->oxl", mixing, pieces, precision=lax.Precision.HIGHEST)

    clique_ids = jnp.arange(clique_count, dtype=jnp.int32)
    sel = [
        (parents[edge][:, None] == clique_ids[None, :]).astype(jnp.float32) for edge in (0, 1)
    ]
    t0, t1, t2 = tables[0, 0], tables[1, 0], tables[2, 0]

    t2_up1 = split_dot(sorting[0], t2)
    (message,), total = send([(t2_up1, 0)], with_slots=True)
    scaled1 = message * (sep_states / total)
    (scaled1_mid,) = to_middle([scaled1])
    (incoming1,), _ = from_middle([jnp.exp(mix(sel[1].T, jnp.log(scaled1_mid)))])
    t0_down0 = split_dot(sorting[2], t0)
    (level0_rows, picked), _ = fetch([(incoming1, 3)], extra=t0_down0)
    down0_message = segment_rows(level0_rows, arrived[2], per_owner)
    t1_down1 = split_dot(sorting[3], t1) * picked
    t1_up0 = split_dot(down1_to_up0, t1_down1)
    (message,), total = send([(t1_up0, 1)])
    scaled0 = message * (sep_states / total)
    scaled0_mid, down0_mid = to_middle([scaled0, down0_message])
    incoming0_mid = jnp.exp(mix(sel[0].T, jnp.log(scaled0_mid)))
    incoming0_mid = jnp.where(jnp.isfinite(incoming0_mid), incoming0_mid, 0.0)
    fresh0_mid = down0_mid * incoming0_mid
    partial = jnp.dot(sel[0], jnp.sum(fresh0_mid, axis=(1, 2)), precision=lax.Precision.HIGHEST)
    update0_mid = mix(sel[0], fresh0_mid) / scaled0_mid
    (update0, incoming0), range_total = from_middle([update0_mid, incoming0_mid], partial)
    (picked, update0), total = fetch([(incoming0, 2), (update0, 1)], range_total)
    out0 = split_dot(sorting[2], t0_down0 * picked, transposed=True)
    t1_up0 = t1_up0 * (update0 * (sep_states / total))
    out1 = split_dot(sorting[1], t1_up0, transposed=True)
    t1_down1 = split_dot(down1_to_up0, t1_up0, transposed=True)
    (message,), total = send([(t1_down1, 3)])
    fresh1 = message * (sep_states / total)
    (fresh1_mid,) = to_middle([fresh1])
    (update1,), _ = from_middle([mix(sel[1], fresh1_mid) / scaled1_mid])
    (picked,), _ = fetch([(update1, 0)])
    out2 = split_dot(sorting[0], t2_up1 * picked, transposed=True)
    return jnp.stack([out0, out1, out2])[:, None]


def solution(mesh):
    return jax.shard_map(
        shards,
        mesh=mesh,
        in_specs=(
            P(None, "clique", "shard", None),
            P(None, "clique", "shard"),
            P(None, "clique", "shard"),
            P(),
        ),
        out_specs=P(None, "clique", "shard", None),
        check_vma=False,
    )
```

```python
import jax
import jax.numpy as jnp
from jax import lax
from jax.sharding import PartitionSpec as P

SEPB = 4096
PAD = 8


def split_dot(one_hot, x, transposed=False):
    lanes = x.shape[-1]
    hi = lax.reduce_precision(x, exponent_bits=8, mantissa_bits=7)
    lo = x - hi
    parts = jnp.concatenate([hi, lo], axis=1).astype(jnp.bfloat16)
    contract = 0 if transposed else 1
    y = lax.dot_general(
        one_hot, parts, (((contract,), (0,)), ((), ())), preferred_element_type=jnp.float32
    )
    return y[:, :lanes] + y[:, lanes:]


def one_hot_of(index, count):
    return (index[:, None] == jnp.arange(count, dtype=jnp.int32)[None, :]).astype(jnp.bfloat16)


def gather_rows(x, index):
    one_hot = (index[:, None] == jnp.arange(x.shape[0], dtype=jnp.int32)[None, :]).astype(
        jnp.bfloat16
    )
    return split_dot(one_hot, x)


def segment_rows(x, segment, count):
    one_hot = (jnp.arange(count, dtype=jnp.int32)[:, None] == segment[None, :]).astype(
        jnp.bfloat16
    )
    return split_dot(one_hot, x)


def shards(tables, up_map, down_map, parents):
    shard_count = lax.axis_size("shard")
    clique_count = lax.axis_size("clique")
    block_count = tables.shape[2]
    lane_count = tables.shape[3]
    per_owner = SEPB // shard_count
    per_peer = block_count // shard_count
    sep_states = float(SEPB * lane_count)

    lists = jnp.stack([up_map[1, 0], up_map[0, 0], down_map[0, 0], down_map[1, 0]])
    owner = lists // per_owner
    slot = lists % per_owner
    owned = (owner[:, :, None] == jnp.arange(shard_count, dtype=jnp.int32)).astype(jnp.bfloat16)
    earlier = (
        jnp.arange(block_count, dtype=jnp.int32)[:, None]
        >= jnp.arange(block_count, dtype=jnp.int32)[None, :]
    ).astype(jnp.bfloat16)
    owned_all = owned.transpose(1, 0, 2).reshape(block_count, 4 * shard_count)
    counts = jnp.dot(earlier, owned_all, preferred_element_type=jnp.float32)
    counts = counts.reshape(block_count, 4, shard_count).transpose(1, 0, 2)
    rank = jnp.sum(counts * owned.astype(jnp.float32), axis=2).astype(jnp.int32) - 1
    position = owner * per_peer + rank
    sorting = [
        (jnp.arange(block_count, dtype=jnp.int32)[:, None] == position[which][None, :]).astype(
            jnp.bfloat16
        )
        for which in range(4)
    ]
    halves = jnp.stack([slot // 32, slot % 32], axis=2).astype(jnp.bfloat16)
    placed = (
        position[:, :, None] == jnp.arange(block_count, dtype=jnp.int32)[None, None, :]
    ).astype(jnp.bfloat16)
    sent_halves = jnp.einsum("lbi,lbh->lih", placed, halves, preferred_element_type=jnp.float32)
    sent_slots = (sent_halves[:, :, 0] * 32 + sent_halves[:, :, 1]).astype(jnp.int32)
    down1_to_up0 = lax.dot_general(
        sorting[1], sorting[3], (((1,), (1,)), ((), ())), preferred_element_type=jnp.float32
    ).astype(jnp.bfloat16)
    slot_rows = (4 * per_peer) // lane_count
    slot_chunk = (
        sent_slots.reshape(4, shard_count, per_peer)
        .transpose(1, 0, 2)
        .reshape(shard_count, slot_rows, lane_count)
        .astype(jnp.float32)
    )
    arrived = [None] * 4
    piece_rows = per_owner // clique_count

    def send(items, with_slots=False):
        partial_sum = jnp.sum(items[0][0])
        chunks = [rows.reshape(shard_count, per_peer, lane_count) for rows, _ in items]
        chunks.append(jnp.broadcast_to(partial_sum, (shard_count, PAD, lane_count)))
        if with_slots:
            chunks.append(slot_chunk)
        arrived_rows = lax.all_to_all(jnp.concatenate(chunks, axis=1), "shard", 0, 0, tiled=True)
        head = len(items) * per_peer
        total = jnp.sum(arrived_rows[:, head, 0])
        if with_slots:
            got = arrived_rows[:, head + PAD :].reshape(shard_count, 4, per_peer)
            got = got.transpose(1, 0, 2).reshape(4, block_count).astype(jnp.int32)
            for which in range(4):
                arrived[which] = got[which]
        messages = []
        for number, (_, which) in enumerate(items):
            rows = arrived_rows[:, number * per_peer : (number + 1) * per_peer]
            messages.append(
                segment_rows(rows.reshape(block_count, lane_count), arrived[which], per_owner)
            )
        return messages, total

    def fetch(items, partial=None, extra=None):
        chunks = [] if extra is None else [extra.reshape(shard_count, per_peer, lane_count)]
        for owned_rows, which in items:
            owned_rows = jnp.where(jnp.isfinite(owned_rows), owned_rows, 0.0)
            picked = gather_rows(owned_rows, arrived[which])
            chunks.append(picked.reshape(shard_count, per_peer, lane_count))
        if partial is not None:
            chunks.append(jnp.broadcast_to(partial, (shard_count, PAD, lane_count)))
        back = lax.all_to_all(jnp.concatenate(chunks, axis=1), "shard", 0, 0, tiled=True)
        count = len(items) + (extra is not None)
        rows = [
            back[:, number * per_peer : (number + 1) * per_peer].reshape(block_count, lane_count)
            for number in range(count)
        ]
        if partial is None:
            return rows, None
        return rows, jnp.sum(back[:, count * per_peer, 0])

    def to_middle(arrays):
        pieces = [a.reshape(clique_count, piece_rows, lane_count) for a in arrays]
        got = lax.all_to_all(jnp.concatenate(pieces, axis=1), "clique", 0, 0, tiled=True)
        return [got[:, n * piece_rows : (n + 1) * piece_rows] for n in range(len(arrays))]

    def from_middle(arrays, partial=None):
        chunks = list(arrays)
        if partial is not None:
            chunks.append(jnp.broadcast_to(partial[:, None, None], (clique_count, PAD, lane_count)))
        got = lax.all_to_all(jnp.concatenate(chunks, axis=1), "clique", 0, 0, tiled=True)
        outs = [
            got[:, n * piece_rows : (n + 1) * piece_rows].reshape(per_owner, lane_count)
            for n in range(len(arrays))
        ]
        if partial is None:
            return outs, None
        return outs, jnp.sum(got[:, len(arrays) * piece_rows, 0])

    def mix(mixing, pieces):
        return jnp.einsum("oi,ixl->oxl", mixing, pieces, precision=lax.Precision.HIGHEST)

    clique_ids = jnp.arange(clique_count, dtype=jnp.int32)
    sel = [
        (parents[edge][:, None] == clique_ids[None, :]).astype(jnp.float32) for edge in (0, 1)
    ]
    t0, t1, t2 = tables[0, 0], tables[1, 0], tables[2, 0]

    t2_up1 = split_dot(sorting[0], t2)
    (message,), total = send([(t2_up1, 0)], with_slots=True)
    scaled1 = message * (sep_states / total)
    (scaled1_mid,) = to_middle([scaled1])
    (incoming1,), _ = from_middle([jnp.exp(mix(sel[1].T, jnp.log(scaled1_mid)))])
    t0_down0 = split_dot(sorting[2], t0)
    (level0_rows, picked), _ = fetch([(incoming1, 3)], extra=t0_down0)
    down0_message = segment_rows(level0_rows, arrived[2], per_owner)
    t1_down1 = split_dot(sorting[3], t1) * picked
    t1_up0 = split_dot(down1_to_up0, t1_down1)
    (message,), total = send([(t1_up0, 1)])
    scaled0 = message * (sep_states / total)
    scaled0_mid, down0_mid = to_middle([scaled0, down0_message])
    incoming0_mid = jnp.exp(mix(sel[0].T, jnp.log(scaled0_mid)))
    incoming0_mid = jnp.where(jnp.isfinite(incoming0_mid), incoming0_mid, 0.0)
    fresh0_mid = down0_mid * incoming0_mid
    partial = jnp.dot(sel[0], jnp.sum(fresh0_mid, axis=(1, 2)), precision=lax.Precision.HIGHEST)
    update0_mid = jnp.take(fresh0_mid, parents[0], axis=0) / scaled0_mid
    (update0, incoming0), range_total = from_middle([update0_mid, incoming0_mid], partial)
    (picked, update0), total = fetch([(incoming0, 2), (update0, 1)], range_total)
    out0 = split_dot(sorting[2], t0_down0 * picked, transposed=True)
    t1_up0 = t1_up0 * (update0 * (sep_states / total))
    out1 = split_dot(sorting[1], t1_up0, transposed=True)
    t1_down1 = split_dot(down1_to_up0, t1_up0, transposed=True)
    (message,), total = send([(t1_down1, 3)])
    fresh1 = message * (sep_states / total)
    (fresh1_mid,) = to_middle([fresh1])
    (update1,), _ = from_middle([jnp.take(fresh1_mid, parents[1], axis=0) / scaled1_mid])
    (picked,), _ = fetch([(update1, 0)])
    out2 = split_dot(sorting[0], t2_up1 * picked, transposed=True)
    return jnp.stack([out0, out1, out2])[:, None]


def solution(mesh):
    return jax.shard_map(
        shards,
        mesh=mesh,
        in_specs=(
            P(None, "clique", "shard", None),
            P(None, "clique", "shard"),
            P(None, "clique", "shard"),
            P(),
        ),
        out_specs=P(None, "clique", "shard", None),
        check_vma=False,
    )
```

```python
import jax
import jax.numpy as jnp
from jax import lax
from jax.sharding import PartitionSpec as P

SEPB = 4096
PAD = 8


def split_dot(one_hot, x, transposed=False):
    lanes = x.shape[-1]
    hi = lax.reduce_precision(x, exponent_bits=8, mantissa_bits=7)
    lo = x - hi
    parts = jnp.concatenate([hi, lo], axis=1).astype(jnp.bfloat16)
    contract = 0 if transposed else 1
    y = lax.dot_general(
        one_hot, parts, (((contract,), (0,)), ((), ())), preferred_element_type=jnp.float32
    )
    return y[:, :lanes] + y[:, lanes:]


def one_hot_of(index, count):
    return (index[:, None] == jnp.arange(count, dtype=jnp.int32)[None, :]).astype(jnp.bfloat16)


def gather_rows(x, index):
    one_hot = (index[:, None] == jnp.arange(x.shape[0], dtype=jnp.int32)[None, :]).astype(
        jnp.bfloat16
    )
    return split_dot(one_hot, x)


def segment_rows(x, segment, count):
    one_hot = (jnp.arange(count, dtype=jnp.int32)[:, None] == segment[None, :]).astype(
        jnp.bfloat16
    )
    return split_dot(one_hot, x)


def shards(tables, up_map, down_map, parents):
    shard_count = lax.axis_size("shard")
    clique_count = lax.axis_size("clique")
    block_count = tables.shape[2]
    lane_count = tables.shape[3]
    per_owner = SEPB // shard_count
    per_peer = block_count // shard_count
    sep_states = float(SEPB * lane_count)

    lists = jnp.stack([up_map[1, 0], up_map[0, 0], down_map[0, 0], down_map[1, 0]])
    owner = lists // per_owner
    slot = lists % per_owner
    owned = (owner[:, :, None] == jnp.arange(shard_count, dtype=jnp.int32)).astype(jnp.bfloat16)
    earlier = (
        jnp.arange(block_count, dtype=jnp.int32)[:, None]
        >= jnp.arange(block_count, dtype=jnp.int32)[None, :]
    ).astype(jnp.bfloat16)
    owned_all = owned.transpose(1, 0, 2).reshape(block_count, 4 * shard_count)
    counts = jnp.dot(earlier, owned_all, preferred_element_type=jnp.float32)
    counts = counts.reshape(block_count, 4, shard_count).transpose(1, 0, 2)
    rank = jnp.sum(counts * owned.astype(jnp.float32), axis=2).astype(jnp.int32) - 1
    position = owner * per_peer + rank
    sorting = [
        (jnp.arange(block_count, dtype=jnp.int32)[:, None] == position[which][None, :]).astype(
            jnp.bfloat16
        )
        for which in range(4)
    ]
    halves = jnp.stack([slot // 32, slot % 32], axis=2).astype(jnp.bfloat16)
    placed = (
        position[:, :, None] == jnp.arange(block_count, dtype=jnp.int32)[None, None, :]
    ).astype(jnp.bfloat16)
    sent_halves = jnp.einsum("lbi,lbh->lih", placed, halves, preferred_element_type=jnp.float32)
    sent_slots = (sent_halves[:, :, 0] * 32 + sent_halves[:, :, 1]).astype(jnp.int32)
    down1_to_up0 = lax.dot_general(
        sorting[1], sorting[3], (((1,), (1,)), ((), ())), preferred_element_type=jnp.float32
    ).astype(jnp.bfloat16)
    slot_rows = (4 * per_peer) // lane_count
    slot_chunk = (
        sent_slots.reshape(4, shard_count, per_peer)
        .transpose(1, 0, 2)
        .reshape(shard_count, slot_rows, lane_count)
        .astype(jnp.float32)
    )
    arrived = [None] * 4
    piece_rows = per_owner // clique_count

    def send(items, with_slots=False, unsorted=None):
        partial_sum = jnp.sum(items[0][0] if unsorted is None else unsorted)
        chunks = [rows.reshape(shard_count, per_peer, lane_count) for rows, _ in items]
        chunks.append(jnp.broadcast_to(partial_sum, (shard_count, PAD, lane_count)))
        if with_slots:
            chunks.append(slot_chunk)
        arrived_rows = lax.all_to_all(jnp.concatenate(chunks, axis=1), "shard", 0, 0, tiled=True)
        head = len(items) * per_peer
        total = jnp.sum(arrived_rows[:, head, 0])
        if with_slots:
            got = arrived_rows[:, head + PAD :].reshape(shard_count, 4, per_peer)
            got = got.transpose(1, 0, 2).reshape(4, block_count).astype(jnp.int32)
            for which in range(4):
                arrived[which] = got[which]
        messages = []
        for number, (_, which) in enumerate(items):
            rows = arrived_rows[:, number * per_peer : (number + 1) * per_peer]
            messages.append(
                segment_rows(rows.reshape(block_count, lane_count), arrived[which], per_owner)
            )
        return messages, total

    def fetch(items, partial=None, extra=None):
        chunks = [] if extra is None else [extra.reshape(shard_count, per_peer, lane_count)]
        for owned_rows, which in items:
            owned_rows = jnp.where(jnp.isfinite(owned_rows), owned_rows, 0.0)
            picked = gather_rows(owned_rows, arrived[which])
            chunks.append(picked.reshape(shard_count, per_peer, lane_count))
        if partial is not None:
            chunks.append(jnp.broadcast_to(partial, (shard_count, PAD, lane_count)))
        back = lax.all_to_all(jnp.concatenate(chunks, axis=1), "shard", 0, 0, tiled=True)
        count = len(items) + (extra is not None)
        rows = [
            back[:, number * per_peer : (number + 1) * per_peer].reshape(block_count, lane_count)
            for number in range(count)
        ]
        if partial is None:
            return rows, None
        return rows, jnp.sum(back[:, count * per_peer, 0])

    def to_middle(arrays):
        pieces = [a.reshape(clique_count, piece_rows, lane_count) for a in arrays]
        got = lax.all_to_all(jnp.concatenate(pieces, axis=1), "clique", 0, 0, tiled=True)
        return [got[:, n * piece_rows : (n + 1) * piece_rows] for n in range(len(arrays))]

    def from_middle(arrays, partial=None):
        chunks = list(arrays)
        if partial is not None:
            chunks.append(jnp.broadcast_to(partial[:, None, None], (clique_count, PAD, lane_count)))
        got = lax.all_to_all(jnp.concatenate(chunks, axis=1), "clique", 0, 0, tiled=True)
        outs = [
            got[:, n * piece_rows : (n + 1) * piece_rows].reshape(per_owner, lane_count)
            for n in range(len(arrays))
        ]
        if partial is None:
            return outs, None
        return outs, jnp.sum(got[:, len(arrays) * piece_rows, 0])

    def mix(mixing, pieces):
        return jnp.einsum("oi,ixl->oxl", mixing, pieces, precision=lax.Precision.HIGHEST)

    clique_ids = jnp.arange(clique_count, dtype=jnp.int32)
    sel = [
        (parents[edge][:, None] == clique_ids[None, :]).astype(jnp.float32) for edge in (0, 1)
    ]
    t0, t1, t2 = tables[0, 0], tables[1, 0], tables[2, 0]

    t2_up1 = split_dot(sorting[0], t2)
    (message,), total = send([(t2_up1, 0)], with_slots=True, unsorted=t2)
    scaled1 = message * (sep_states / total)
    (scaled1_mid,) = to_middle([scaled1])
    (incoming1,), _ = from_middle([jnp.exp(mix(sel[1].T, jnp.log(scaled1_mid)))])
    t0_down0 = split_dot(sorting[2], t0)
    (level0_rows, picked), _ = fetch([(incoming1, 3)], extra=t0_down0)
    down0_message = segment_rows(level0_rows, arrived[2], per_owner)
    t1_down1 = split_dot(sorting[3], t1) * picked
    t1_up0 = split_dot(down1_to_up0, t1_down1)
    (message,), total = send([(t1_up0, 1)], unsorted=t1_down1)
    scaled0 = message * (sep_states / total)
    scaled0_mid, down0_mid = to_middle([scaled0, down0_message])
    incoming0_mid = jnp.exp(mix(sel[0].T, jnp.log(scaled0_mid)))
    incoming0_mid = jnp.where(jnp.isfinite(incoming0_mid), incoming0_mid, 0.0)
    fresh0_mid = down0_mid * incoming0_mid
    partial = jnp.dot(sel[0], jnp.sum(fresh0_mid, axis=(1, 2)), precision=lax.Precision.HIGHEST)
    update0_mid = mix(sel[0], fresh0_mid) / scaled0_mid
    (update0, incoming0), range_total = from_middle([update0_mid, incoming0_mid], partial)
    (picked, update0), total = fetch([(incoming0, 2), (update0, 1)], range_total)
    out0 = split_dot(sorting[2], t0_down0 * picked, transposed=True)
    t1_up0 = t1_up0 * (update0 * (sep_states / total))
    out1 = split_dot(sorting[1], t1_up0, transposed=True)
    t1_down1 = split_dot(down1_to_up0, t1_up0, transposed=True)
    (message,), total = send([(t1_down1, 3)], unsorted=t1_up0)
    fresh1 = message * (sep_states / total)
    (fresh1_mid,) = to_middle([fresh1])
    (update1,), _ = from_middle([mix(sel[1], fresh1_mid) / scaled1_mid])
    (picked,), _ = fetch([(update1, 0)])
    out2 = split_dot(sorting[0], t2_up1 * picked, transposed=True)
    return jnp.stack([out0, out1, out2])[:, None]


def solution(mesh):
    return jax.shard_map(
        shards,
        mesh=mesh,
        in_specs=(
            P(None, "clique", "shard", None),
            P(None, "clique", "shard"),
            P(None, "clique", "shard"),
            P(),
        ),
        out_specs=P(None, "clique", "shard", None),
        check_vma=False,
    )
```

```python
import jax
import jax.numpy as jnp
from jax import lax
from jax.sharding import PartitionSpec as P

SEPB = 4096
PAD = 8


def split_dot(one_hot, x, transposed=False):
    lanes = x.shape[-1]
    hi = lax.reduce_precision(x, exponent_bits=8, mantissa_bits=7)
    lo = x - hi
    parts = jnp.concatenate([hi, lo], axis=1).astype(jnp.bfloat16)
    contract = 0 if transposed else 1
    y = lax.dot_general(
        one_hot, parts, (((contract,), (0,)), ((), ())), preferred_element_type=jnp.float32
    )
    return y[:, :lanes] + y[:, lanes:]


def one_hot_of(index, count):
    return (index[:, None] == jnp.arange(count, dtype=jnp.int32)[None, :]).astype(jnp.bfloat16)


def gather_rows(x, index):
    one_hot = (index[:, None] == jnp.arange(x.shape[0], dtype=jnp.int32)[None, :]).astype(
        jnp.bfloat16
    )
    return split_dot(one_hot, x)


def segment_rows(x, segment, count):
    one_hot = (jnp.arange(count, dtype=jnp.int32)[:, None] == segment[None, :]).astype(
        jnp.bfloat16
    )
    return split_dot(one_hot, x)


def shards(tables, up_map, down_map, parents):
    shard_count = lax.axis_size("shard")
    clique_count = lax.axis_size("clique")
    block_count = tables.shape[2]
    lane_count = tables.shape[3]
    per_owner = SEPB // shard_count
    per_peer = block_count // shard_count
    sep_states = float(SEPB * lane_count)

    lists = jnp.stack([up_map[1, 0], up_map[0, 0], down_map[0, 0], down_map[1, 0]])
    owner = lists // per_owner
    slot = lists % per_owner
    owned = (owner[:, :, None] == jnp.arange(shard_count, dtype=jnp.int32)).astype(jnp.bfloat16)
    earlier = (
        jnp.arange(block_count, dtype=jnp.int32)[:, None]
        >= jnp.arange(block_count, dtype=jnp.int32)[None, :]
    ).astype(jnp.bfloat16)
    owned_all = owned.transpose(1, 0, 2).reshape(block_count, 4 * shard_count)
    counts = jnp.dot(earlier, owned_all, preferred_element_type=jnp.float32)
    counts = counts.reshape(block_count, 4, shard_count).transpose(1, 0, 2)
    rank = jnp.sum(counts * owned.astype(jnp.float32), axis=2).astype(jnp.int32) - 1
    position = owner * per_peer + rank
    sorting = [
        (jnp.arange(block_count, dtype=jnp.int32)[:, None] == position[which][None, :]).astype(
            jnp.bfloat16
        )
        for which in range(4)
    ]
    halves = jnp.stack([slot // 32, slot % 32], axis=2).astype(jnp.bfloat16)
    placed = (
        position[:, :, None] == jnp.arange(block_count, dtype=jnp.int32)[None, None, :]
    ).astype(jnp.bfloat16)
    sent_halves = jnp.einsum("lbi,lbh->lih", placed, halves, preferred_element_type=jnp.float32)
    sent_slots = (sent_halves[:, :, 0] * 32 + sent_halves[:, :, 1]).astype(jnp.int32)
    down1_to_up0 = lax.dot_general(
        sorting[1], sorting[3], (((1,), (1,)), ((), ())), preferred_element_type=jnp.float32
    ).astype(jnp.bfloat16)
    slot_rows = (4 * per_peer) // lane_count
    slot_chunk = (
        sent_slots.reshape(4, shard_count, per_peer)
        .transpose(1, 0, 2)
        .reshape(shard_count, slot_rows, lane_count)
        .astype(jnp.float32)
    )
    arrived = [None] * 4
    piece_rows = per_owner // clique_count

    def send(items, with_slots=False):
        partial_sum = jnp.sum(items[0][0])
        chunks = [rows.reshape(shard_count, per_peer, lane_count) for rows, _ in items]
        chunks.append(jnp.broadcast_to(partial_sum, (shard_count, PAD, lane_count)))
        if with_slots:
            chunks.append(slot_chunk)
        arrived_rows = lax.all_to_all(jnp.concatenate(chunks, axis=1), "shard", 0, 0, tiled=True)
        head = len(items) * per_peer
        total = jnp.sum(arrived_rows[:, head, 0])
        if with_slots:
            got = arrived_rows[:, head + PAD :].reshape(shard_count, 4, per_peer)
            got = got.transpose(1, 0, 2).reshape(4, block_count).astype(jnp.int32)
            for which in range(4):
                arrived[which] = got[which]
        messages = []
        for number, (_, which) in enumerate(items):
            rows = arrived_rows[:, number * per_peer : (number + 1) * per_peer]
            messages.append(
                segment_rows(rows.reshape(block_count, lane_count), arrived[which], per_owner)
            )
        return messages, total

    def fetch(items, partial=None, extra=None):
        chunks = [] if extra is None else [extra.reshape(shard_count, per_peer, lane_count)]
        for owned_rows, which in items:
            if which != 2:
                owned_rows = jnp.where(jnp.isfinite(owned_rows), owned_rows, 0.0)
            picked = gather_rows(owned_rows, arrived[which])
            chunks.append(picked.reshape(shard_count, per_peer, lane_count))
        if partial is not None:
            chunks.append(jnp.broadcast_to(partial, (shard_count, PAD, lane_count)))
        back = lax.all_to_all(jnp.concatenate(chunks, axis=1), "shard", 0, 0, tiled=True)
        count = len(items) + (extra is not None)
        rows = [
            back[:, number * per_peer : (number + 1) * per_peer].reshape(block_count, lane_count)
            for number in range(count)
        ]
        if partial is None:
            return rows, None
        return rows, jnp.sum(back[:, count * per_peer, 0])

    def to_middle(arrays):
        pieces = [a.reshape(clique_count, piece_rows, lane_count) for a in arrays]
        got = lax.all_to_all(jnp.concatenate(pieces, axis=1), "clique", 0, 0, tiled=True)
        return [got[:, n * piece_rows : (n + 1) * piece_rows] for n in range(len(arrays))]

    def from_middle(arrays, partial=None):
        chunks = list(arrays)
        if partial is not None:
            chunks.append(jnp.broadcast_to(partial[:, None, None], (clique_count, PAD, lane_count)))
        got = lax.all_to_all(jnp.concatenate(chunks, axis=1), "clique", 0, 0, tiled=True)
        outs = [
            got[:, n * piece_rows : (n + 1) * piece_rows].reshape(per_owner, lane_count)
            for n in range(len(arrays))
        ]
        if partial is None:
            return outs, None
        return outs, jnp.sum(got[:, len(arrays) * piece_rows, 0])

    def mix(mixing, pieces):
        return jnp.einsum("oi,ixl->oxl", mixing, pieces, precision=lax.Precision.HIGHEST)

    clique_ids = jnp.arange(clique_count, dtype=jnp.int32)
    sel = [
        (parents[edge][:, None] == clique_ids[None, :]).astype(jnp.float32) for edge in (0, 1)
    ]
    t0, t1, t2 = tables[0, 0], tables[1, 0], tables[2, 0]

    t2_up1 = split_dot(sorting[0], t2)
    (message,), total = send([(t2_up1, 0)], with_slots=True)
    scaled1 = message * (sep_states / total)
    (scaled1_mid,) = to_middle([scaled1])
    (incoming1,), _ = from_middle([jnp.exp(mix(sel[1].T, jnp.log(scaled1_mid)))])
    t0_down0 = split_dot(sorting[2], t0)
    (level0_rows, picked), _ = fetch([(incoming1, 3)], extra=t0_down0)
    down0_message = segment_rows(level0_rows, arrived[2], per_owner)
    t1_down1 = split_dot(sorting[3], t1) * picked
    t1_up0 = split_dot(down1_to_up0, t1_down1)
    (message,), total = send([(t1_up0, 1)])
    scaled0 = message * (sep_states / total)
    scaled0_mid, down0_mid = to_middle([scaled0, down0_message])
    incoming0_mid = jnp.exp(mix(sel[0].T, jnp.log(scaled0_mid)))
    incoming0_mid = jnp.where(jnp.isfinite(incoming0_mid), incoming0_mid, 0.0)
    fresh0_mid = down0_mid * incoming0_mid
    partial = jnp.dot(sel[0], jnp.sum(fresh0_mid, axis=(1, 2)), precision=lax.Precision.HIGHEST)
    update0_mid = mix(sel[0], fresh0_mid) / scaled0_mid
    (update0, incoming0), range_total = from_middle([update0_mid, incoming0_mid], partial)
    (picked, update0), total = fetch([(incoming0, 2), (update0, 1)], range_total)
    out0 = split_dot(sorting[2], t0_down0 * picked, transposed=True)
    t1_up0 = t1_up0 * (update0 * (sep_states / total))
    out1 = split_dot(sorting[1], t1_up0, transposed=True)
    t1_down1 = split_dot(down1_to_up0, t1_up0, transposed=True)
    (message,), total = send([(t1_down1, 3)])
    fresh1 = message * (sep_states / total)
    (fresh1_mid,) = to_middle([fresh1])
    (update1,), _ = from_middle([mix(sel[1], fresh1_mid) / scaled1_mid])
    (picked,), _ = fetch([(update1, 0)])
    out2 = split_dot(sorting[0], t2_up1 * picked, transposed=True)
    return jnp.stack([out0, out1, out2])[:, None]


def solution(mesh):
    return jax.shard_map(
        shards,
        mesh=mesh,
        in_specs=(
            P(None, "clique", "shard", None),
            P(None, "clique", "shard"),
            P(None, "clique", "shard"),
            P(),
        ),
        out_specs=P(None, "clique", "shard", None),
        check_vma=False,
    )
```
